256 devices in a mesh: req: 128 (over z, y, x), tensor: 2 (over core).
Axes of the slice: x: 4, y: 4, z: 8, core: 2. Of those that a mesh axis runs over, the one named last changes fastest.
Arguments:
- patches: bfloat16 [256, 256, 1280], P('req'), may hold values from -6 to 6
- grids: int32 [256, 2], replicated, may hold values from 2 to 16, as said below
- place: int32 [256], replicated, may hold values from 0 to 255, as said below
- text_tokens: bfloat16 [128, 384, 1280], P('req'), may hold values from -6 to 6
- encoder_attend_in: bfloat16 [1280, 3, 1280], P(None, None, 'tensor'), may hold values from -0.15625 to 0.15625
- encoder_attend_out: bfloat16 [1280, 1280], P('tensor'), may hold values from -0.15625 to 0.15625
- encoder_expand: bfloat16 [1280, 5120], P(None, 'tensor'), may hold values from -0.15625 to 0.15625
- encoder_contract: bfloat16 [5120, 1280], P('tensor'), may hold values from -0.078125 to 0.078125
- encoder_gain_first: float32 [1280], replicated, may hold values from 0.25 to 1.75
- encoder_gain_second: float32 [1280], replicated, may hold values from 0.25 to 1.75
- merge_weight: bfloat16 [5120, 1280], P(None, 'tensor'), may hold values from -0.078125 to 0.078125
- decoder_attend_in: bfloat16 [1280, 3, 1280], P(None, None, 'tensor'), may hold values from -0.15625 to 0.15625
- decoder_attend_out: bfloat16 [1280, 1280], P('tensor'), may hold values from -0.15625 to 0.15625
- decoder_expand: bfloat16 [1280, 5120], P(None, 'tensor'), may hold values from -0.15625 to 0.15625
- decoder_contract: bfloat16 [5120, 1280], P('tensor'), may hold values from -0.078125 to 0.078125
- decoder_gain_first: float32 [1280], replicated, may hold values from 0.25 to 1.75
- decoder_gain_second: float32 [1280], replicated, may hold values from 0.25 to 1.75
Outputs:
- decoded: bfloat16 [128, 512, 1280], P('req')
The draws below stay inside these ranges and needn't reach their ends.
Inputs may be any that keep to these rules, and one draw needn't show every extreme that they name: `grids`: both entries are even; image 0 always has the full 16 x 16 grid. A permutation: image i's merged tokens go to request place[i] // 2, image slot place[i] % 2. The request index, taken bitwise exclusive-or with i // 2, depends on i % 2 only: it is 1 when i % 2 = 0 and 64 when i % 2 = 1.
All inputs are finite; a program needn't handle non-finite values.
Results may differ from the reference program's by a relative error of at most 0.015.
Values may be sent and summed in bfloat16 or wider, within the bound.
No kernel may reach another device: no remote copies, remote signals or barrier semaphores. Data moves between devices by JAX's collectives and lax.ppermute only.
A program may use at most 192 MiB of HBM per device.

```python
import jax
import jax.numpy as jnp
from jax import lax

D = 1280
HEAD_DIM = 80
FF = 5120
GRID = 16
IMG_DEV = 2
TEXT = 384
PAD = 256
REQUESTS = 128
IMAGES = 256


def draw_grids(key, part):
    sides = 2 * jax.random.randint(key, (IMAGES, 2), 1, GRID // 2 + 1)
    return sides.at[0].set(GRID).astype(jnp.int32)


def draw_place(key, part):
    count = IMAGES // IMG_DEV
    first, second = jax.random.split(jax.random.fold_in(key, 7), 2)
    shuffled = jax.random.permutation(first, count).astype(jnp.int32)
    order_key = jnp.where(shuffled == 1, -2, jnp.where(shuffled == count // 2, -1, jnp.arange(count, dtype=jnp.int32))).astype(jnp.int32)
    order = jnp.argsort(order_key, stable=True)
    masks = shuffled[order][:IMG_DEV].astype(jnp.int32)
    source = jnp.arange(count, dtype=jnp.int32)
    within = jnp.arange(IMG_DEV, dtype=jnp.int32)
    target = jnp.bitwise_xor(source[:, None], masks[None, :])
    rotate = jax.random.randint(second, (count,), 0, IMG_DEV).astype(jnp.int32)
    slot = (within[None, :] + rotate[target]) % IMG_DEV
    return (target * IMG_DEV + slot).reshape(IMAGES).astype(jnp.int32)


def block_scale(key, shape, cuts, smallest, high):
    factor_of, own = 1.0, jax.random.fold_in(key, 6)
    for dim, parts in cuts:
        steps = jnp.exp(jax.random.uniform(jax.random.fold_in(own, dim), (parts,), jnp.float32, smallest / len(cuts), high / len(cuts)))
        factor_of = factor_of * jnp.repeat(steps, shape[dim] // parts).reshape([-1 if axis == dim else 1 for axis in range(len(shape))])
    return factor_of


def bell_draw(own_key, dims, scale, limit, shards=(), kind=jnp.bfloat16):
    result = jax.random.normal(own_key, dims, jnp.float32) * scale
    if len(shards) > 0:
        result = block_scale(own_key, dims, shards, -0.22, 0.18) * result
    return jnp.clip(result, min=-limit, max=limit).astype(kind)


def setup_inputs(seed: int = 0) -> dict:
    key_of = jax.random.split(jax.random.key(seed), 18)
    patches = bell_draw(key_of[0], (IMAGES, PAD, D), 1.0, 6.0, ((0, 128),))
    grids = draw_grids(jax.random.fold_in(key_of[17], 71), 0)
    place = draw_place(jax.random.fold_in(key_of[17], 71), 0)
    text_tokens = bell_draw(key_of[3], (REQUESTS, TEXT, D), 1.0, 6.0, ((0, 128),))
    encoder_attend_in = bell_draw(key_of[4], (D, 3, D), D ** -0.5, 0.15625, ((2, 2),))
    encoder_attend_out = bell_draw(key_of[5], (D, D), D ** -0.5, 0.15625, ((0, 2),))
    encoder_expand = bell_draw(key_of[6], (D, FF), D ** -0.5, 0.15625, ((1, 2),))
    encoder_contract = bell_draw(key_of[7], (FF, D), FF ** -0.5, 0.078125, ((0, 2),))
    encoder_gain_first = jnp.clip(1.0 + 0.15 * jax.random.normal(key_of[8], (D,), jnp.float32), 0.25, 1.75)
    encoder_gain_second = jnp.clip(1.0 + 0.15 * jax.random.normal(key_of[9], (D,), jnp.float32), 0.25, 1.75)
    merge_weight = bell_draw(key_of[10], (4 * D, D), (4 * D) ** -0.5, 0.078125, ((1, 2),))
    decoder_attend_in = bell_draw(key_of[11], (D, 3, D), D ** -0.5, 0.15625, ((2, 2),))
    decoder_attend_out = bell_draw(key_of[12], (D, D), D ** -0.5, 0.15625, ((0, 2),))
    decoder_expand = bell_draw(key_of[13], (D, FF), D ** -0.5, 0.15625, ((1, 2),))
    decoder_contract = bell_draw(key_of[14], (FF, D), FF ** -0.5, 0.078125, ((0, 2),))
    decoder_gain_first = jnp.clip(1.0 + 0.15 * jax.random.normal(key_of[15], (D,), jnp.float32), 0.25, 1.75)
    decoder_gain_second = jnp.clip(1.0 + 0.15 * jax.random.normal(key_of[16], (D,), jnp.float32), 0.25, 1.75)
    return {"patches": patches, "grids": grids, "place": place, "text_tokens": text_tokens, "encoder_attend_in": encoder_attend_in, "encoder_attend_out": encoder_attend_out, "encoder_expand": encoder_expand, "encoder_contract": encoder_contract, "encoder_gain_first": encoder_gain_first, "encoder_gain_second": encoder_gain_second, "merge_weight": merge_weight, "decoder_attend_in": decoder_attend_in, "decoder_attend_out": decoder_attend_out, "decoder_expand": decoder_expand, "decoder_contract": decoder_contract, "decoder_gain_first": decoder_gain_first, "decoder_gain_second": decoder_gain_second}


def normalize(values, gain):
    center = values - lax.optimization_barrier(jnp.mean(values, axis=-1, keepdims=True))
    spread = lax.optimization_barrier(jnp.mean(center * center, axis=-1, keepdims=True))
    return center * lax.rsqrt(spread + 1e-06) * gain

def attend(normed, key_valid, causal, attend_in, attend_out):
    length = normed.shape[0]
    width = attend_in.shape[0]
    projected = jnp.dot(normed, attend_in.reshape(width, -1), preferred_element_type=jnp.float32).astype(jnp.bfloat16)
    projected = projected.reshape(length, 3, -1, HEAD_DIM)
    queries = projected[:, 0].astype(jnp.float32)
    key_rows = projected[:, 1].astype(jnp.float32)
    value_rows = projected[:, 2].astype(jnp.float32)
    scores = jnp.einsum('qhd,khd->hqk', queries, key_rows) * HEAD_DIM ** (-0.5)
    allowed = jnp.broadcast_to(key_valid[None, :], (length, length))
    if causal:
        positions = jnp.arange(length)
        allowed = allowed & (positions[None, :] <= positions[:, None])
    scores = jnp.where(allowed[None], scores, jnp.float32(-1e+30))
    probs = jax.nn.softmax(scores, axis=-1).astype(jnp.bfloat16)
    mixed = jnp.einsum('hqk,khd->qhd', probs.astype(jnp.float32), value_rows).astype(jnp.bfloat16)
    return jnp.dot(mixed.reshape(length, -1), attend_out, preferred_element_type=jnp.float32)

def layer(inputs, key_valid, causal, attend_in, attend_out, expand, contract, gain_first, gain_second):
    widened = inputs.astype(jnp.float32)
    first = normalize(widened, gain_first).astype(jnp.bfloat16)
    residual = widened + attend(first, key_valid, causal, attend_in, attend_out)
    second = normalize(residual, gain_second).astype(jnp.bfloat16)
    hidden = jax.nn.gelu(jnp.dot(second, expand, preferred_element_type=jnp.float32), approximate=False).astype(jnp.bfloat16)
    return (residual + jnp.dot(hidden, contract, preferred_element_type=jnp.float32)).astype(jnp.bfloat16)

def reference(patches, grids, place, text_tokens, encoder_attend_in, encoder_attend_out, encoder_expand, encoder_contract, encoder_gain_first, encoder_gain_second, merge_weight, decoder_attend_in, decoder_attend_out, decoder_expand, decoder_contract, decoder_gain_first, decoder_gain_second):
    cells = jnp.arange(GRID * GRID)
    cell_rows = cells // GRID
    cell_cols = cells % GRID

    def encode(pair):
        image, grid = pair
        valid = (cell_rows < grid[0]) & (cell_cols < grid[1])
        return layer(image, valid, False, encoder_attend_in, encoder_attend_out, encoder_expand, encoder_contract, encoder_gain_first, encoder_gain_second)
    encoded = lax.map(encode, (patches, grids))
    half = GRID // 2
    blocks = encoded.reshape(IMAGES, half, 2, half, 2, D).transpose(0, 1, 3, 2, 4, 5).reshape(IMAGES, half * half, 4 * D)
    merged = lax.map(lambda block: jnp.dot(block, merge_weight, preferred_element_type=jnp.float32).astype(jnp.bfloat16), blocks)
    slots = jnp.arange(half * half)
    merged_valid = ((2 * (slots // half))[None, :] < grids[:, 0:1]) & ((2 * (slots % half))[None, :] < grids[:, 1:2])
    inverse = jnp.zeros((IMAGES,), jnp.int32).at[place].set(jnp.arange(IMAGES, dtype=jnp.int32))
    arranged = merged[inverse].reshape(REQUESTS, IMG_DEV * half * half, D)
    arranged_valid = merged_valid[inverse].reshape(REQUESTS, IMG_DEV * half * half)
    prompts = jnp.concatenate([arranged, text_tokens], axis=1)
    prompt_valid = jnp.concatenate([arranged_valid, jnp.ones((REQUESTS, TEXT), bool)], axis=1)

    def decode(pair):
        prompt, valid = pair
        return layer(prompt, valid, True, decoder_attend_in, decoder_attend_out, decoder_expand, decoder_contract, decoder_gain_first, decoder_gain_second)
    decoded = lax.map(decode, (prompts, prompt_valid))
    return jnp.where(prompt_valid[..., None], decoded, jnp.zeros_like(decoded))
```

```python
import jax
import jax.numpy as jnp
from jax import lax
from jax.sharding import PartitionSpec as P

HEAD_DIM = 80
GRID = 16
REQ_XOR = (1, 64)


def normalize(values, gain):
    center = values - jnp.mean(values, axis=-1, keepdims=True)
    spread = jnp.mean(center * center, axis=-1, keepdims=True)
    return center * lax.rsqrt(spread + 1e-06) * gain


def tensor_sum(partial):
    mine = partial.astype(jnp.bfloat16)
    other = lax.ppermute(mine, "tensor", [(0, 1), (1, 0)])
    return mine.astype(jnp.float32) + other.astype(jnp.float32)


def attend(normed, allowed, attend_in, attend_out):
    batch, length, width = normed.shape
    projected = jnp.einsum(
        "bld,dkf->blkf", normed, attend_in, preferred_element_type=jnp.float32
    ).astype(jnp.bfloat16)
    projected = projected.reshape(batch, length, 3, -1, HEAD_DIM)
    queries = projected[:, :, 0]
    key_rows = projected[:, :, 1]
    value_rows = projected[:, :, 2]
    scores = jnp.einsum(
        "bqhd,bkhd->bhqk", queries, key_rows, preferred_element_type=jnp.float32
    ) * HEAD_DIM ** (-0.5)
    scores = jnp.where(allowed[:, None], scores, jnp.float32(-1e30))
    probs = jax.nn.softmax(scores, axis=-1).astype(jnp.bfloat16)
    mixed = jnp.einsum(
        "bhqk,bkhd->bqhd", probs, value_rows, preferred_element_type=jnp.float32
    ).astype(jnp.bfloat16)
    return jnp.dot(mixed.reshape(batch, length, -1), attend_out, preferred_element_type=jnp.float32)


def layer(inputs, allowed, attend_in, attend_out, expand, contract, gain_first, gain_second):
    widened = inputs.astype(jnp.float32)
    first = normalize(widened, gain_first).astype(jnp.bfloat16)
    attended = attend(first, allowed, attend_in, attend_out)
    residual = widened + tensor_sum(attended)
    second = normalize(residual, gain_second).astype(jnp.bfloat16)
    hidden = jax.nn.gelu(
        jnp.dot(second, expand, preferred_element_type=jnp.float32), approximate=False
    ).astype(jnp.bfloat16)
    partial_out = jnp.dot(hidden, contract, preferred_element_type=jnp.float32)
    return (residual + tensor_sum(partial_out)).astype(jnp.bfloat16)


def on_device(
    req_count,
    patches,
    grids,
    place,
    text_tokens,
    encoder_attend_in,
    encoder_attend_out,
    encoder_expand,
    encoder_contract,
    encoder_gain_first,
    encoder_gain_second,
    merge_weight,
    decoder_attend_in,
    decoder_attend_out,
    decoder_expand,
    decoder_contract,
    decoder_gain_first,
    decoder_gain_second,
):
    device = lax.axis_index("req")
    core = lax.axis_index("tensor")
    images_here, cell_count, width = patches.shape
    side = GRID
    half = side // 2
    slot_count = half * half
    local_grids = lax.dynamic_slice_in_dim(grids, device * images_here, images_here, 0)
    cells = jnp.arange(cell_count)
    cell_valid = ((cells // side)[None, :] < local_grids[:, 0:1]) & (
        (cells % side)[None, :] < local_grids[:, 1:2]
    )
    image_allowed = jnp.broadcast_to(cell_valid[:, None, :], (images_here, cell_count, cell_count))
    encoded = layer(
        patches,
        image_allowed,
        encoder_attend_in,
        encoder_attend_out,
        encoder_expand,
        encoder_contract,
        encoder_gain_first,
        encoder_gain_second,
    )
    blocks = (
        encoded.reshape(images_here, half, 2, half, 2, width)
        .transpose(0, 1, 3, 2, 4, 5)
        .reshape(images_here * slot_count, 4 * width)
    )
    merged = jnp.dot(blocks, merge_weight, preferred_element_type=jnp.float32).astype(jnp.bfloat16)
    merged = merged.reshape(images_here, slot_count, -1)

    arrived = []
    for j in range(images_here):
        halves = []
        for flip in (0, 1):
            perm = [
                (r * 2 + t, (r ^ REQ_XOR[j]) * 2 + (t ^ flip))
                for r in range(req_count)
                for t in range(2)
            ]
            halves.append(lax.ppermute(merged[j], ("req", "tensor"), perm))
        same, other = halves
        low = jnp.where(core == 0, same, other)
        high = jnp.where(core == 0, other, same)
        arrived.append(jnp.concatenate([low, high], axis=-1))
    sources = [(device ^ REQ_XOR[j]) * images_here + j for j in range(images_here)]
    first_slot = place[sources[0]] % 2
    swap = first_slot != 0
    image_rows = jnp.where(
        swap,
        jnp.concatenate([arrived[1], arrived[0]], axis=0),
        jnp.concatenate([arrived[0], arrived[1]], axis=0),
    )
    grid_a = grids[sources[0]]
    grid_b = grids[sources[1]]
    slot_grids = jnp.where(swap, jnp.stack([grid_b, grid_a]), jnp.stack([grid_a, grid_b]))
    slots = jnp.arange(slot_count)
    merged_valid = ((2 * (slots // half))[None, :] < slot_grids[:, 0:1]) & (
        (2 * (slots % half))[None, :] < slot_grids[:, 1:2]
    )
    prompt = jnp.concatenate([image_rows, text_tokens[0]], axis=0)[None]
    text_count = text_tokens.shape[1]
    prompt_valid = jnp.concatenate(
        [merged_valid.reshape(-1), jnp.ones((text_count,), bool)], axis=0
    )
    length = prompt.shape[1]
    positions = jnp.arange(length)
    prompt_allowed = (prompt_valid[None, :] & (positions[None, :] <= positions[:, None]))[None]
    decoded = layer(
        prompt,
        prompt_allowed,
        decoder_attend_in,
        decoder_attend_out,
        decoder_expand,
        decoder_contract,
        decoder_gain_first,
        decoder_gain_second,
    )
    return jnp.where(prompt_valid[None, :, None], decoded, jnp.zeros_like(decoded))


def solution(mesh):
    placed = (
        P("req", None, None),
        P(),
        P(),
        P("req", None, None),
        P(None, None, "tensor"),
        P("tensor", None),
        P(None, "tensor"),
        P("tensor", None),
        P(),
        P(),
        P(None, "tensor"),
        P(None, None, "tensor"),
        P("tensor", None),
        P(None, "tensor"),
        P("tensor", None),
        P(),
        P(),
    )

    def body(*args):
        return on_device(mesh.shape["req"], *args)

    return jax.shard_map(
        body, mesh=mesh, in_specs=placed, out_specs=P("req", None, None), check_vma=False
    )
```

```python
import jax
import jax.numpy as jnp
from jax import lax
from jax.sharding import PartitionSpec as P

HEAD_DIM = 80
GRID = 16
REQ_XOR = (1, 64)


def normalize(values, gain):
    center = values - jnp.mean(values, axis=-1, keepdims=True)
    spread = jnp.mean(center * center, axis=-1, keepdims=True)
    return center * lax.rsqrt(spread + 1e-06) * gain


def tensor_sum(partial):
    mine = partial.astype(jnp.bfloat16)
    other = lax.ppermute(mine, "tensor", [(0, 1), (1, 0)])
    return mine.astype(jnp.float32) + other.astype(jnp.float32)


def attend(normed, allowed, attend_in, attend_out):
    batch, length, width = normed.shape
    projected = jnp.einsum(
        "bld,dkf->blkf", normed, attend_in, preferred_element_type=jnp.float32
    ).astype(jnp.bfloat16)
    projected = projected.reshape(batch, length, 3, -1, HEAD_DIM)
    queries = projected[:, :, 0]
    key_rows = projected[:, :, 1]
    value_rows = projected[:, :, 2]
    scores = jnp.einsum(
        "bqhd,bkhd->bhqk", queries, key_rows, preferred_element_type=jnp.float32
    ) * HEAD_DIM ** (-0.5)
    scores = jnp.where(allowed[:, None], scores, jnp.float32(-1e30))
    probs = jax.nn.softmax(scores, axis=-1).astype(jnp.bfloat16)
    mixed = jnp.einsum(
        "bhqk,bkhd->bqhd", probs, value_rows, preferred_element_type=jnp.float32
    ).astype(jnp.bfloat16)
    return jnp.dot(mixed.reshape(batch, length, -1), attend_out, preferred_element_type=jnp.float32)


def layer(inputs, allowed, attend_in, attend_out, expand, contract, gain_first, gain_second):
    widened = inputs.astype(jnp.float32)
    first = lax.optimization_barrier(normalize(widened, gain_first).astype(jnp.bfloat16))
    attended = attend(first, allowed, attend_in, attend_out)
    residual = widened + tensor_sum(attended)
    second = lax.optimization_barrier(normalize(residual, gain_second).astype(jnp.bfloat16))
    hidden = jax.nn.gelu(
        jnp.dot(second, expand, preferred_element_type=jnp.float32), approximate=False
    ).astype(jnp.bfloat16)
    hidden = lax.optimization_barrier(hidden)
    partial_out = jnp.dot(hidden, contract, preferred_element_type=jnp.float32)
    return (residual + tensor_sum(partial_out)).astype(jnp.bfloat16)


def on_device(
    req_count,
    patches,
    grids,
    place,
    text_tokens,
    encoder_attend_in,
    encoder_attend_out,
    encoder_expand,
    encoder_contract,
    encoder_gain_first,
    encoder_gain_second,
    merge_weight,
    decoder_attend_in,
    decoder_attend_out,
    decoder_expand,
    decoder_contract,
    decoder_gain_first,
    decoder_gain_second,
):
    device = lax.axis_index("req")
    core = lax.axis_index("tensor")
    images_here, cell_count, width = patches.shape
    side = GRID
    half = side // 2
    slot_count = half * half
    local_grids = lax.dynamic_slice_in_dim(grids, device * images_here, images_here, 0)
    order = jnp.arange(cell_count).reshape(half, 2, half, 2).transpose(0, 2, 1, 3).reshape(-1)
    cell_rows = order // side
    cell_cols = order % side
    cell_valid = (cell_rows[None, :] < local_grids[:, 0:1]) & (cell_cols[None, :] < local_grids[:, 1:2])
    image_allowed = jnp.broadcast_to(cell_valid[:, None, :], (images_here, cell_count, cell_count))
    blocked = (
        patches.reshape(images_here, half, 2, half, 2, width)
        .transpose(0, 1, 3, 2, 4, 5)
        .reshape(images_here, cell_count, width)
    )
    encoded = layer(
        blocked,
        image_allowed,
        encoder_attend_in,
        encoder_attend_out,
        encoder_expand,
        encoder_contract,
        encoder_gain_first,
        encoder_gain_second,
    )
    blocks = encoded.reshape(images_here * slot_count, 4 * width)
    merged = jnp.dot(blocks, merge_weight, preferred_element_type=jnp.float32).astype(jnp.bfloat16)
    merged = merged.reshape(images_here, slot_count, -1)

    arrived = []
    for j in range(images_here):
        halves = []
        for flip in (0, 1):
            perm = [
                (r * 2 + t, (r ^ REQ_XOR[j]) * 2 + (t ^ flip))
                for r in range(req_count)
                for t in range(2)
            ]
            halves.append(lax.ppermute(merged[j], ("req", "tensor"), perm))
        same, other = halves
        low = jnp.where(core == 0, same, other)
        high = jnp.where(core == 0, other, same)
        arrived.append(jnp.concatenate([low, high], axis=-1))
    sources = [(device ^ REQ_XOR[j]) * images_here + j for j in range(images_here)]
    first_slot = place[sources[0]] % 2
    swap = first_slot != 0
    image_rows = jnp.where(
        swap,
        jnp.concatenate([arrived[1], arrived[0]], axis=0),
        jnp.concatenate([arrived[0], arrived[1]], axis=0),
    )
    grid_a = grids[sources[0]]
    grid_b = grids[sources[1]]
    slot_grids = jnp.where(swap, jnp.stack([grid_b, grid_a]), jnp.stack([grid_a, grid_b]))
    slots = jnp.arange(slot_count)
    merged_valid = ((2 * (slots // half))[None, :] < slot_grids[:, 0:1]) & (
        (2 * (slots % half))[None, :] < slot_grids[:, 1:2]
    )
    prompt = jnp.concatenate([image_rows, text_tokens[0]], axis=0)[None]
    text_count = text_tokens.shape[1]
    prompt_valid = jnp.concatenate(
        [merged_valid.reshape(-1), jnp.ones((text_count,), bool)], axis=0
    )
    length = prompt.shape[1]
    positions = jnp.arange(length)
    prompt_allowed = (prompt_valid[None, :] & (positions[None, :] <= positions[:, None]))[None]
    decoded = layer(
        prompt,
        prompt_allowed,
        decoder_attend_in,
        decoder_attend_out,
        decoder_expand,
        decoder_contract,
        decoder_gain_first,
        decoder_gain_second,
    )
    return jnp.where(prompt_valid[None, :, None], decoded, jnp.zeros_like(decoded))


def solution(mesh):
    placed = (
        P("req", None, None),
        P(),
        P(),
        P("req", None, None),
        P(None, None, "tensor"),
        P("tensor", None),
        P(None, "tensor"),
        P("tensor", None),
        P(),
        P(),
        P(None, "tensor"),
        P(None, None, "tensor"),
        P("tensor", None),
        P(None, "tensor"),
        P("tensor", None),
        P(),
        P(),
    )

    def body(*args):
        return on_device(mesh.shape["req"], *args)

    return jax.shard_map(
        body, mesh=mesh, in_specs=placed, out_specs=P("req", None, None), check_vma=False
    )
```

```python
import jax
import jax.numpy as jnp
from jax import lax
from jax.sharding import PartitionSpec as P

HEAD_DIM = 80
GRID = 16
REQ_XOR = (1, 64)


def normalize(values, gain):
    center = values - jnp.mean(values, axis=-1, keepdims=True)
    spread = jnp.mean(center * center, axis=-1, keepdims=True)
    return center * lax.rsqrt(spread + 1e-06) * gain


def tensor_sum(partial):
    mine = partial.astype(jnp.bfloat16)
    other = lax.ppermute(mine, "tensor", [(0, 1), (1, 0)])
    return mine.astype(jnp.float32) + other.astype(jnp.float32)


def project(widened, attend_in, gain_first):
    first = lax.optimization_barrier(normalize(widened, gain_first).astype(jnp.bfloat16))
    return jnp.einsum(
        "ld,dkf->lkf", first, attend_in, preferred_element_type=jnp.float32
    ).astype(jnp.bfloat16)


def attend(projected, allowed):
    length = projected.shape[0]
    projected = projected.reshape(length, 3, -1, HEAD_DIM)
    queries = projected[:, 0]
    key_rows = projected[:, 1]
    value_rows = projected[:, 2]
    scores = jnp.einsum(
        "qhd,khd->hqk", queries, key_rows, preferred_element_type=jnp.float32
    ) * HEAD_DIM ** (-0.5)
    scores = jnp.where(allowed[None], scores, jnp.float32(-1e30))
    probs = jax.nn.softmax(scores, axis=-1).astype(jnp.bfloat16)
    mixed = jnp.einsum(
        "hqk,khd->qhd", probs, value_rows, preferred_element_type=jnp.float32
    ).astype(jnp.bfloat16)
    return mixed.reshape(length, -1)


def finish(widened, mixed, attend_out, expand, contract, gain_second):
    residual = widened + tensor_sum(
        jnp.dot(mixed, attend_out, preferred_element_type=jnp.float32)
    )
    second = lax.optimization_barrier(normalize(residual, gain_second).astype(jnp.bfloat16))
    hidden = jax.nn.gelu(
        jnp.dot(second, expand, preferred_element_type=jnp.float32), approximate=False
    ).astype(jnp.bfloat16)
    hidden = lax.optimization_barrier(hidden)
    partial_out = jnp.dot(hidden, contract, preferred_element_type=jnp.float32)
    return (residual + tensor_sum(partial_out)).astype(jnp.bfloat16)


def layer_rest(widened, projected, allowed, weights, chunks):
    attend_out, expand, contract, gain_second = weights
    mixed = attend(projected, allowed)
    rows = widened.shape[0] // chunks
    outs = [
        finish(
            widened[c * rows : (c + 1) * rows],
            mixed[c * rows : (c + 1) * rows],
            attend_out,
            expand,
            contract,
            gain_second,
        )
        for c in range(chunks)
    ]
    return jnp.concatenate(outs, axis=0)


def on_device(
    req_count,
    patches,
    grids,
    place,
    text_tokens,
    encoder_attend_in,
    encoder_attend_out,
    encoder_expand,
    encoder_contract,
    encoder_gain_first,
    encoder_gain_second,
    merge_weight,
    decoder_attend_in,
    decoder_attend_out,
    decoder_expand,
    decoder_contract,
    decoder_gain_first,
    decoder_gain_second,
):
    device = lax.axis_index("req")
    core = lax.axis_index("tensor")
    images_here, cell_count, width = patches.shape
    side = GRID
    half = side // 2
    slot_count = half * half
    local_grids = lax.dynamic_slice_in_dim(grids, device * images_here, images_here, 0)
    cells = jnp.arange(cell_count)
    cell_valid = ((cells // side)[None, :] < local_grids[:, 0:1]) & (
        (cells % side)[None, :] < local_grids[:, 1:2]
    )
    encoder_rest = (encoder_attend_out, encoder_expand, encoder_contract, encoder_gain_second)
    encoded_images = []
    for j in range(images_here):
        widened = patches[j].astype(jnp.float32)
        projected = project(widened, encoder_attend_in, encoder_gain_first)
        allowed = jnp.broadcast_to(cell_valid[j][None, :], (cell_count, cell_count))
        encoded_images.append(layer_rest(widened, projected, allowed, encoder_rest, 1))
    encoded = jnp.stack(encoded_images)
    blocks = (
        encoded.reshape(images_here, half, 2, half, 2, width)
        .transpose(0, 1, 3, 2, 4, 5)
        .reshape(images_here * slot_count, 4 * width)
    )
    merged = jnp.dot(blocks, merge_weight, preferred_element_type=jnp.float32).astype(jnp.bfloat16)
    merged = merged.reshape(images_here, slot_count, -1)

    arrived = []
    for j in range(images_here):
        halves = []
        for flip in (0, 1):
            perm = [
                (r * 2 + t, (r ^ REQ_XOR[j]) * 2 + (t ^ flip))
                for r in range(req_count)
                for t in range(2)
            ]
            halves.append(lax.ppermute(merged[j], ("req", "tensor"), perm))
        same, other = halves
        low = jnp.where(core == 0, same, other)
        high = jnp.where(core == 0, other, same)
        arrived.append(jnp.concatenate([low, high], axis=-1))
    sources = [(device ^ REQ_XOR[j]) * images_here + j for j in range(images_here)]
    first_slot = place[sources[0]] % 2
    swap = first_slot != 0
    image_rows = jnp.where(
        swap,
        jnp.concatenate([arrived[1], arrived[0]], axis=0),
        jnp.concatenate([arrived[0], arrived[1]], axis=0),
    )
    grid_a = grids[sources[0]]
    grid_b = grids[sources[1]]
    slot_grids = jnp.where(swap, jnp.stack([grid_b, grid_a]), jnp.stack([grid_a, grid_b]))
    slots = jnp.arange(slot_count)
    merged_valid = ((2 * (slots // half))[None, :] < slot_grids[:, 0:1]) & (
        (2 * (slots % half))[None, :] < slot_grids[:, 1:2]
    )
    text_widened = text_tokens[0].astype(jnp.float32)
    text_projected = project(text_widened, decoder_attend_in, decoder_gain_first)
    image_widened = image_rows.astype(jnp.float32)
    image_projected = project(image_widened, decoder_attend_in, decoder_gain_first)
    widened = jnp.concatenate([image_widened, text_widened], axis=0)
    projected = jnp.concatenate([image_projected, text_projected], axis=0)
    text_count = text_tokens.shape[1]
    prompt_valid = jnp.concatenate(
        [merged_valid.reshape(-1), jnp.ones((text_count,), bool)], axis=0
    )
    length = widened.shape[0]
    positions = jnp.arange(length)
    prompt_allowed = prompt_valid[None, :] & (positions[None, :] <= positions[:, None])
    decoder_rest = (decoder_attend_out, decoder_expand, decoder_contract, decoder_gain_second)
    decoded = layer_rest(widened, projected, prompt_allowed, decoder_rest, 2)[None]
    return jnp.where(prompt_valid[None, :, None], decoded, jnp.zeros_like(decoded))


def solution(mesh):
    placed = (
        P("req", None, None),
        P(),
        P(),
        P("req", None, None),
        P(None, None, "tensor"),
        P("tensor", None),
        P(None, "tensor"),
        P("tensor", None),
        P(),
        P(),
        P(None, "tensor"),
        P(None, None, "tensor"),
        P("tensor", None),
        P(None, "tensor"),
        P("tensor", None),
        P(),
        P(),
    )

    def body(*args):
        return on_device(mesh.shape["req"], *args)

    return jax.shard_map(
        body, mesh=mesh, in_specs=placed, out_specs=P("req", None, None), check_vma=False
    )
```

```python
import functools

import jax
import jax.numpy as jnp
from jax import lax
from jax.experimental import pallas as pl
from jax.experimental.pallas import tpu as pltpu
from jax.sharding import PartitionSpec as P

HEAD_DIM = 80
GRID = 16
REQ_XOR = (1, 64)


def normalize(values, gain):
    center = values - jnp.mean(values, axis=-1, keepdims=True)
    spread = jnp.mean(center * center, axis=-1, keepdims=True)
    return center * lax.rsqrt(spread + 1e-06) * gain


def tensor_sum(partial):
    mine = partial.astype(jnp.bfloat16)
    other = lax.ppermute(mine, "tensor", [(0, 1), (1, 0)])
    return mine.astype(jnp.float32) + other.astype(jnp.float32)


def _feed_forward_kernel(rows_per_step, x_ref, w1_ref, w2_ref, o_ref, acc_ref):
    k = pl.program_id(0)

    @pl.when(k == 0)
    def _():
        acc_ref[...] = jnp.zeros_like(acc_ref)

    w1 = w1_ref[...]
    w2 = w2_ref[...]
    for r in range(x_ref.shape[0] // rows_per_step):
        rows = pl.ds(r * rows_per_step, rows_per_step)
        h = jnp.dot(x_ref[rows, :], w1, preferred_element_type=jnp.float32)
        g = (h * 0.5 * (1.0 + lax.erf(h * (2.0 ** -0.5)))).astype(jnp.bfloat16)
        acc_ref[rows, :] += jnp.dot(g, w2, preferred_element_type=jnp.float32)

    @pl.when(k == pl.num_programs(0) - 1)
    def _():
        o_ref[...] = acc_ref[...].astype(o_ref.dtype)


def feed_forward(x, expand, contract, hidden_step=512, rows_per_step=128):
    length, width = x.shape
    hidden = expand.shape[1]
    return pl.pallas_call(
        functools.partial(_feed_forward_kernel, rows_per_step),
        out_shape=jax.ShapeDtypeStruct((length, width), jnp.bfloat16),
        grid=(hidden // hidden_step,),
        in_specs=[
            pl.BlockSpec((length, width), lambda k: (0, 0)),
            pl.BlockSpec((width, hidden_step), lambda k: (0, k)),
            pl.BlockSpec((hidden_step, width), lambda k: (k, 0)),
        ],
        out_specs=pl.BlockSpec((length, width), lambda k: (0, 0)),
        scratch_shapes=[pltpu.VMEM((length, width), jnp.float32)],
        cost_estimate=pl.CostEstimate(
            flops=4 * length * width * hidden,
            transcendentals=length * hidden,
            bytes_accessed=2 * (2 * width * hidden + 2 * length * width),
        ),
    )(x, expand, contract)


def attend(normed, allowed, attend_in, attend_out):
    batch, length, width = normed.shape
    projected = jnp.einsum(
        "bld,dkf->blkf", normed, attend_in, preferred_element_type=jnp.float32
    ).astype(jnp.bfloat16)
    projected = projected.reshape(batch, length, 3, -1, HEAD_DIM)
    queries = projected[:, :, 0]
    key_rows = projected[:, :, 1]
    value_rows = projected[:, :, 2]
    scores = jnp.einsum(
        "bqhd,bkhd->bhqk", queries, key_rows, preferred_element_type=jnp.float32
    ) * HEAD_DIM ** (-0.5)
    scores = jnp.where(allowed[:, None], scores, jnp.float32(-1e30))
    probs = jax.nn.softmax(scores, axis=-1).astype(jnp.bfloat16)
    mixed = jnp.einsum(
        "bhqk,bkhd->bqhd", probs, value_rows, preferred_element_type=jnp.float32
    ).astype(jnp.bfloat16)
    return jnp.dot(mixed.reshape(batch, length, -1), attend_out, preferred_element_type=jnp.float32)


def layer(inputs, allowed, attend_in, attend_out, expand, contract, gain_first, gain_second):
    widened = inputs.astype(jnp.float32)
    first = lax.optimization_barrier(normalize(widened, gain_first).astype(jnp.bfloat16))
    attended = attend(first, allowed, attend_in, attend_out)
    residual = widened + tensor_sum(attended)
    second = normalize(residual, gain_second).astype(jnp.bfloat16)
    batch, length, width = second.shape
    partial_out = feed_forward(second.reshape(batch * length, width), expand, contract)
    return (residual + tensor_sum(partial_out.reshape(batch, length, width))).astype(jnp.bfloat16)


def on_device(
    req_count,
    patches,
    grids,
    place,
    text_tokens,
    encoder_attend_in,
    encoder_attend_out,
    encoder_expand,
    encoder_contract,
    encoder_gain_first,
    encoder_gain_second,
    merge_weight,
    decoder_attend_in,
    decoder_attend_out,
    decoder_expand,
    decoder_contract,
    decoder_gain_first,
    decoder_gain_second,
):
    device = lax.axis_index("req")
    core = lax.axis_index("tensor")
    images_here, cell_count, width = patches.shape
    side = GRID
    half = side // 2
    slot_count = half * half
    local_grids = lax.dynamic_slice_in_dim(grids, device * images_here, images_here, 0)
    cells = jnp.arange(cell_count)
    cell_valid = ((cells // side)[None, :] < local_grids[:, 0:1]) & (
        (cells % side)[None, :] < local_grids[:, 1:2]
    )
    image_allowed = jnp.broadcast_to(cell_valid[:, None, :], (images_here, cell_count, cell_count))
    encoded = layer(
        patches,
        image_allowed,
        encoder_attend_in,
        encoder_attend_out,
        encoder_expand,
        encoder_contract,
        encoder_gain_first,
        encoder_gain_second,
    )
    blocks = (
        encoded.reshape(images_here, half, 2, half, 2, width)
        .transpose(0, 1, 3, 2, 4, 5)
        .reshape(images_here * slot_count, 4 * width)
    )
    merged = jnp.dot(blocks, merge_weight, preferred_element_type=jnp.float32).astype(jnp.bfloat16)
    merged = merged.reshape(images_here, slot_count, -1)

    arrived = []
    for j in range(images_here):
        halves = []
        for flip in (0, 1):
            perm = [
                (r * 2 + t, (r ^ REQ_XOR[j]) * 2 + (t ^ flip))
                for r in range(req_count)
                for t in range(2)
            ]
            halves.append(lax.ppermute(merged[j], ("req", "tensor"), perm))
        same, other = halves
        low = jnp.where(core == 0, same, other)
        high = jnp.where(core == 0, other, same)
        arrived.append(jnp.concatenate([low, high], axis=-1))
    sources = [(device ^ REQ_XOR[j]) * images_here + j for j in range(images_here)]
    first_slot = place[sources[0]] % 2
    swap = first_slot != 0
    image_rows = jnp.where(
        swap,
        jnp.concatenate([arrived[1], arrived[0]], axis=0),
        jnp.concatenate([arrived[0], arrived[1]], axis=0),
    )
    grid_a = grids[sources[0]]
    grid_b = grids[sources[1]]
    slot_grids = jnp.where(swap, jnp.stack([grid_b, grid_a]), jnp.stack([grid_a, grid_b]))
    slots = jnp.arange(slot_count)
    merged_valid = ((2 * (slots // half))[None, :] < slot_grids[:, 0:1]) & (
        (2 * (slots % half))[None, :] < slot_grids[:, 1:2]
    )
    prompt = jnp.concatenate([image_rows, text_tokens[0]], axis=0)[None]
    text_count = text_tokens.shape[1]
    prompt_valid = jnp.concatenate(
        [merged_valid.reshape(-1), jnp.ones((text_count,), bool)], axis=0
    )
    length = prompt.shape[1]
    positions = jnp.arange(length)
    prompt_allowed = (prompt_valid[None, :] & (positions[None, :] <= positions[:, None]))[None]
    decoded = layer(
        prompt,
        prompt_allowed,
        decoder_attend_in,
        decoder_attend_out,
        decoder_expand,
        decoder_contract,
        decoder_gain_first,
        decoder_gain_second,
    )
    return jnp.where(prompt_valid[None, :, None], decoded, jnp.zeros_like(decoded))


def solution(mesh):
    placed = (
        P("req", None, None),
        P(),
        P(),
        P("req", None, None),
        P(None, None, "tensor"),
        P("tensor", None),
        P(None, "tensor"),
        P("tensor", None),
        P(),
        P(),
        P(None, "tensor"),
        P(None, None, "tensor"),
        P("tensor", None),
        P(None, "tensor"),
        P("tensor", None),
        P(),
        P(),
    )

    def body(*args):
        return on_device(mesh.shape["req"], *args)

    return jax.shard_map(
        body, mesh=mesh, in_specs=placed, out_specs=P("req", None, None), check_vma=False
    )
```

```python
import functools

import jax
import jax.numpy as jnp
from jax import lax
from jax.experimental import pallas as pl
from jax.experimental.pallas import tpu as pltpu
from jax.sharding import PartitionSpec as P

HEAD_DIM = 80
GRID = 16
REQ_XOR = (1, 64)


def normalize(values, gain):
    center = values - jnp.mean(values, axis=-1, keepdims=True)
    spread = jnp.mean(center * center, axis=-1, keepdims=True)
    return center * lax.rsqrt(spread + 1e-06) * gain


def tensor_sum(partial):
    mine = partial.astype(jnp.bfloat16)
    other = lax.ppermute(mine, "tensor", [(0, 1), (1, 0)])
    return mine.astype(jnp.float32) + other.astype(jnp.float32)


def _feed_forward_kernel(rows_per_step, x_ref, w1_ref, w2_ref, o_ref, acc_ref):
    k = pl.program_id(0)

    @pl.when(k == 0)
    def _():
        acc_ref[...] = jnp.zeros_like(acc_ref)

    w1 = w1_ref[...]
    w2 = w2_ref[...]
    for r in range(x_ref.shape[0] // rows_per_step):
        rows = pl.ds(r * rows_per_step, rows_per_step)
        h = jnp.dot(x_ref[rows, :], w1, preferred_element_type=jnp.float32)
        g = (h * 0.5 * (1.0 + lax.erf(h * (2.0 ** -0.5)))).astype(jnp.bfloat16)
        acc_ref[rows, :] += jnp.dot(g, w2, preferred_element_type=jnp.float32)

    @pl.when(k == pl.num_programs(0) - 1)
    def _():
        o_ref[...] = acc_ref[...].astype(o_ref.dtype)


def feed_forward(x, expand, contract, hidden_step=512, rows_per_step=128):
    length, width = x.shape
    hidden = expand.shape[1]
    return pl.pallas_call(
        functools.partial(_feed_forward_kernel, rows_per_step),
        out_shape=jax.ShapeDtypeStruct((length, width), jnp.bfloat16),
        grid=(hidden // hidden_step,),
        in_specs=[
            pl.BlockSpec((length, width), lambda k: (0, 0)),
            pl.BlockSpec((width, hidden_step), lambda k: (0, k)),
            pl.BlockSpec((hidden_step, width), lambda k: (k, 0)),
        ],
        out_specs=pl.BlockSpec((length, width), lambda k: (0, 0)),
        scratch_shapes=[pltpu.VMEM((length, width), jnp.float32)],
        cost_estimate=pl.CostEstimate(
            flops=4 * length * width * hidden,
            transcendentals=length * hidden,
            bytes_accessed=2 * (2 * width * hidden + 2 * length * width),
        ),
    )(x, expand, contract)


def _merge_kernel(res_ref, mine_ref, other_ref, w_ref, o_ref):
    cells, width = res_ref.shape[1], res_ref.shape[2]
    half = GRID // 2
    slot = lax.broadcasted_iota(jnp.int32, (half * half, cells), 0)
    cell = lax.broadcasted_iota(jnp.int32, (half * half, cells), 1)
    for i in range(res_ref.shape[0]):
        encoded = (
            res_ref[i] + (mine_ref[i].astype(jnp.float32) + other_ref[i].astype(jnp.float32))
        ).astype(jnp.bfloat16)
        total = None
        for a in range(2):
            for b in range(2):
                wanted = (2 * (slot // half) + a) * GRID + 2 * (slot % half) + b
                pick = jnp.where(cell == wanted, 1.0, 0.0).astype(jnp.bfloat16)
                rows = jnp.dot(pick, encoded, preferred_element_type=jnp.float32).astype(jnp.bfloat16)
                part = jnp.dot(
                    rows,
                    w_ref[pl.ds((2 * a + b) * width, width), :],
                    preferred_element_type=jnp.float32,
                )
                total = part if total is None else total + part
        o_ref[i] = total.astype(o_ref.dtype)


def merge(residual, mine, other, merge_weight):
    images, cells, width = residual.shape
    half = GRID // 2
    out_width = merge_weight.shape[1]
    return pl.pallas_call(
        _merge_kernel,
        out_shape=jax.ShapeDtypeStruct((images, half * half, out_width), jnp.bfloat16),
        cost_estimate=pl.CostEstimate(
            flops=2 * images * cells * width * (out_width + half * half),
            transcendentals=0,
            bytes_accessed=images * cells * width * 8 + merge_weight.size * 2,
        ),
    )(residual, mine, other, merge_weight)


def attend(normed, allowed, attend_in, attend_out):
    batch, length, width = normed.shape
    projected = jnp.einsum(
        "bld,dkf->blkf", normed, attend_in, preferred_element_type=jnp.float32
    ).astype(jnp.bfloat16)
    projected = projected.reshape(batch, length, 3, -1, HEAD_DIM)
    queries = projected[:, :, 0]
    key_rows = projected[:, :, 1]
    value_rows = projected[:, :, 2]
    scores = jnp.einsum(
        "bqhd,bkhd->bhqk", queries, key_rows, preferred_element_type=jnp.float32
    ) * HEAD_DIM ** (-0.5)
    scores = jnp.where(allowed[:, None], scores, jnp.float32(-1e30))
    probs = jax.nn.softmax(scores, axis=-1).astype(jnp.bfloat16)
    mixed = jnp.einsum(
        "bhqk,bkhd->bqhd", probs, value_rows, preferred_element_type=jnp.float32
    ).astype(jnp.bfloat16)
    return jnp.dot(mixed.reshape(batch, length, -1), attend_out, preferred_element_type=jnp.float32)


def layer(inputs, allowed, attend_in, attend_out, expand, contract, gain_first, gain_second, split=False):
    widened = inputs.astype(jnp.float32)
    first = lax.optimization_barrier(normalize(widened, gain_first).astype(jnp.bfloat16))
    attended = attend(first, allowed, attend_in, attend_out)
    residual = widened + tensor_sum(attended)
    second = normalize(residual, gain_second).astype(jnp.bfloat16)
    batch, length, width = second.shape
    partial_out = feed_forward(second.reshape(batch * length, width), expand, contract)
    mine = partial_out.reshape(batch, length, width)
    other = lax.ppermute(mine, "tensor", [(0, 1), (1, 0)])
    if split:
        return residual, mine, other
    return (residual + (mine.astype(jnp.float32) + other.astype(jnp.float32))).astype(jnp.bfloat16)


def on_device(
    req_count,
    patches,
    grids,
    place,
    text_tokens,
    encoder_attend_in,
    encoder_attend_out,
    encoder_expand,
    encoder_contract,
    encoder_gain_first,
    encoder_gain_second,
    merge_weight,
    decoder_attend_in,
    decoder_attend_out,
    decoder_expand,
    decoder_contract,
    decoder_gain_first,
    decoder_gain_second,
):
    device = lax.axis_index("req")
    core = lax.axis_index("tensor")
    images_here, cell_count, width = patches.shape
    side = GRID
    half = side // 2
    slot_count = half * half
    local_grids = lax.dynamic_slice_in_dim(grids, device * images_here, images_here, 0)
    cells = jnp.arange(cell_count)
    cell_valid = ((cells // side)[None, :] < local_grids[:, 0:1]) & (
        (cells % side)[None, :] < local_grids[:, 1:2]
    )
    image_allowed = jnp.broadcast_to(cell_valid[:, None, :], (images_here, cell_count, cell_count))
    residual, mine, other = layer(
        patches,
        image_allowed,
        encoder_attend_in,
        encoder_attend_out,
        encoder_expand,
        encoder_contract,
        encoder_gain_first,
        encoder_gain_second,
        split=True,
    )
    merged = merge(residual, mine, other, merge_weight)

    arrived = []
    for j in range(images_here):
        halves = []
        for flip in (0, 1):
            perm = [
                (r * 2 + t, (r ^ REQ_XOR[j]) * 2 + (t ^ flip))
                for r in range(req_count)
                for t in range(2)
            ]
            halves.append(lax.ppermute(merged[j], ("req", "tensor"), perm))
        same, other = halves
        low = jnp.where(core == 0, same, other)
        high = jnp.where(core == 0, other, same)
        arrived.append(jnp.concatenate([low, high], axis=-1))
    sources = [(device ^ REQ_XOR[j]) * images_here + j for j in range(images_here)]
    first_slot = place[sources[0]] % 2
    swap = first_slot != 0
    image_rows = jnp.where(
        swap,
        jnp.concatenate([arrived[1], arrived[0]], axis=0),
        jnp.concatenate([arrived[0], arrived[1]], axis=0),
    )
    grid_a = grids[sources[0]]
    grid_b = grids[sources[1]]
    slot_grids = jnp.where(swap, jnp.stack([grid_b, grid_a]), jnp.stack([grid_a, grid_b]))
    slots = jnp.arange(slot_count)
    merged_valid = ((2 * (slots // half))[None, :] < slot_grids[:, 0:1]) & (
        (2 * (slots % half))[None, :] < slot_grids[:, 1:2]
    )
    prompt = jnp.concatenate([image_rows, text_tokens[0]], axis=0)[None]
    text_count = text_tokens.shape[1]
    prompt_valid = jnp.concatenate(
        [merged_valid.reshape(-1), jnp.ones((text_count,), bool)], axis=0
    )
    length = prompt.shape[1]
    positions = jnp.arange(length)
    prompt_allowed = (prompt_valid[None, :] & (positions[None, :] <= positions[:, None]))[None]
    decoded = layer(
        prompt,
        prompt_allowed,
        decoder_attend_in,
        decoder_attend_out,
        decoder_expand,
        decoder_contract,
        decoder_gain_first,
        decoder_gain_second,
    )
    return jnp.where(prompt_valid[None, :, None], decoded, jnp.zeros_like(decoded))


def solution(mesh):
    placed = (
        P("req", None, None),
        P(),
        P(),
        P("req", None, None),
        P(None, None, "tensor"),
        P("tensor", None),
        P(None, "tensor"),
        P("tensor", None),
        P(),
        P(),
        P(None, "tensor"),
        P(None, None, "tensor"),
        P("tensor", None),
        P(None, "tensor"),
        P("tensor", None),
        P(),
        P(),
    )

    def body(*args):
        return on_device(mesh.shape["req"], *args)

    return jax.shard_map(
        body, mesh=mesh, in_specs=placed, out_specs=P("req", None, None), check_vma=False
    )
```

```python
import functools

import jax
import jax.numpy as jnp
from jax import lax
from jax.experimental import pallas as pl
from jax.experimental.pallas import tpu as pltpu
from jax.sharding import PartitionSpec as P

HEAD_DIM = 80
GRID = 16
REQ_XOR = (1, 64)


def normalize(values, gain):
    center = values - jnp.mean(values, axis=-1, keepdims=True)
    spread = jnp.mean(center * center, axis=-1, keepdims=True)
    return center * lax.rsqrt(spread + 1e-06) * gain


def tensor_sum(partial):
    mine = partial.astype(jnp.bfloat16)
    other = lax.ppermute(mine, "tensor", [(0, 1), (1, 0)])
    return mine.astype(jnp.float32) + other.astype(jnp.float32)


def _feed_forward_kernel(rows_per_step, res_ref, gain_ref, w1_ref, w2_ref, o_ref, x_ref, acc_ref):
    k = pl.program_id(0)

    @pl.when(k == 0)
    def _():
        values = res_ref[...]
        center = values - jnp.mean(values, axis=-1, keepdims=True)
        spread = jnp.mean(center * center, axis=-1, keepdims=True)
        x_ref[...] = (center * lax.rsqrt(spread + 1e-06) * gain_ref[...]).astype(x_ref.dtype)
        acc_ref[...] = jnp.zeros_like(acc_ref)

    w1 = w1_ref[...]
    w2 = w2_ref[...]
    for r in range(x_ref.shape[0] // rows_per_step):
        rows = pl.ds(r * rows_per_step, rows_per_step)
        h = jnp.dot(x_ref[rows, :], w1, preferred_element_type=jnp.float32)
        g = (h * 0.5 * (1.0 + lax.erf(h * (2.0 ** -0.5)))).astype(jnp.bfloat16)
        acc_ref[rows, :] += jnp.dot(g, w2, preferred_element_type=jnp.float32)

    @pl.when(k == pl.num_programs(0) - 1)
    def _():
        o_ref[...] = acc_ref[...].astype(o_ref.dtype)


def feed_forward(residual, gain, expand, contract, hidden_step=512, rows_per_step=128):
    length, width = residual.shape
    hidden = expand.shape[1]
    return pl.pallas_call(
        functools.partial(_feed_forward_kernel, rows_per_step),
        out_shape=jax.ShapeDtypeStruct((length, width), jnp.bfloat16),
        grid=(hidden // hidden_step,),
        in_specs=[
            pl.BlockSpec((length, width), lambda k: (0, 0)),
            pl.BlockSpec((1, width), lambda k: (0, 0)),
            pl.BlockSpec((width, hidden_step), lambda k: (0, k)),
            pl.BlockSpec((hidden_step, width), lambda k: (k, 0)),
        ],
        out_specs=pl.BlockSpec((length, width), lambda k: (0, 0)),
        scratch_shapes=[
            pltpu.VMEM((length, width), jnp.bfloat16),
            pltpu.VMEM((length, width), jnp.float32),
        ],
        cost_estimate=pl.CostEstimate(
            flops=4 * length * width * hidden,
            transcendentals=length * hidden,
            bytes_accessed=2 * (2 * width * hidden + 3 * length * width),
        ),
    )(residual, gain.reshape(1, width), expand, contract)


def _merge_kernel(res_ref, mine_ref, other_ref, w_ref, o_ref, enc_ref, acc_ref):
    step = pl.program_id(0)
    images, cells = res_ref.shape[0], res_ref.shape[1]
    half = GRID // 2

    @pl.when(step == 0)
    def _():
        for i in range(images):
            enc_ref[i] = (
                res_ref[i] + (mine_ref[i].astype(jnp.float32) + other_ref[i].astype(jnp.float32))
            ).astype(enc_ref.dtype)
        acc_ref[...] = jnp.zeros_like(acc_ref)

    slot = lax.broadcasted_iota(jnp.int32, (half * half, cells), 0)
    cell = lax.broadcasted_iota(jnp.int32, (half * half, cells), 1)
    wanted = (2 * (slot // half) + step // 2) * GRID + 2 * (slot % half) + step % 2
    pick = jnp.where(cell == wanted, 1.0, 0.0).astype(jnp.bfloat16)
    weight = w_ref[...]
    for i in range(images):
        rows = jnp.dot(pick, enc_ref[i], preferred_element_type=jnp.float32).astype(jnp.bfloat16)
        acc_ref[i] += jnp.dot(rows, weight, preferred_element_type=jnp.float32)

    @pl.when(step == pl.num_programs(0) - 1)
    def _():
        o_ref[...] = acc_ref[...].astype(o_ref.dtype)


def merge(residual, mine, other, merge_weight):
    images, cells, width = residual.shape
    half = GRID // 2
    out_width = merge_weight.shape[1]
    whole = pl.BlockSpec((images, cells, width), lambda s: (0, 0, 0))
    return pl.pallas_call(
        _merge_kernel,
        out_shape=jax.ShapeDtypeStruct((images, half * half, out_width), jnp.bfloat16),
        grid=(4,),
        in_specs=[whole, whole, whole, pl.BlockSpec((width, out_width), lambda s: (s, 0))],
        out_specs=pl.BlockSpec((images, half * half, out_width), lambda s: (0, 0, 0)),
        scratch_shapes=[
            pltpu.VMEM((images, cells, width), jnp.bfloat16),
            pltpu.VMEM((images, half * half, out_width), jnp.float32),
        ],
        cost_estimate=pl.CostEstimate(
            flops=2 * images * cells * width * (out_width + half * half),
            transcendentals=0,
            bytes_accessed=images * cells * width * 8 + merge_weight.size * 2,
        ),
    )(residual, mine, other, merge_weight)


def attend(normed, allowed, attend_in, attend_out):
    batch, length, width = normed.shape
    projected = jnp.einsum(
        "bld,dkf->blkf", normed, attend_in, preferred_element_type=jnp.float32
    ).astype(jnp.bfloat16)
    projected = projected.reshape(batch, length, 3, -1, HEAD_DIM)
    queries = projected[:, :, 0]
    key_rows = projected[:, :, 1]
    value_rows = projected[:, :, 2]
    scores = jnp.einsum(
        "bqhd,bkhd->bhqk", queries, key_rows, preferred_element_type=jnp.float32
    ) * HEAD_DIM ** (-0.5)
    scores = jnp.where(allowed[:, None], scores, jnp.float32(-1e30))
    probs = jax.nn.softmax(scores, axis=-1).astype(jnp.bfloat16)
    mixed = jnp.einsum(
        "bhqk,bkhd->bqhd", probs, value_rows, preferred_element_type=jnp.float32
    ).astype(jnp.bfloat16)
    return jnp.dot(mixed.reshape(batch, length, -1), attend_out, preferred_element_type=jnp.float32)


def layer(inputs, allowed, attend_in, attend_out, expand, contract, gain_first, gain_second, split=False):
    widened = inputs.astype(jnp.float32)
    first = lax.optimization_barrier(normalize(widened, gain_first).astype(jnp.bfloat16))
    attended = attend(first, allowed, attend_in, attend_out)
    residual = widened + tensor_sum(attended)
    batch, length, width = residual.shape
    partial_out = feed_forward(residual.reshape(batch * length, width), gain_second, expand, contract)
    mine = partial_out.reshape(batch, length, width)
    other = lax.ppermute(mine, "tensor", [(0, 1), (1, 0)])
    if split:
        return residual, mine, other
    return (residual + (mine.astype(jnp.float32) + other.astype(jnp.float32))).astype(jnp.bfloat16)


def on_device(
    req_count,
    patches,
    grids,
    place,
    text_tokens,
    encoder_attend_in,
    encoder_attend_out,
    encoder_expand,
    encoder_contract,
    encoder_gain_first,
    encoder_gain_second,
    merge_weight,
    decoder_attend_in,
    decoder_attend_out,
    decoder_expand,
    decoder_contract,
    decoder_gain_first,
    decoder_gain_second,
):
    device = lax.axis_index("req")
    core = lax.axis_index("tensor")
    images_here, cell_count, width = patches.shape
    side = GRID
    half = side // 2
    slot_count = half * half
    local_grids = lax.dynamic_slice_in_dim(grids, device * images_here, images_here, 0)
    cells = jnp.arange(cell_count)
    cell_valid = ((cells // side)[None, :] < local_grids[:, 0:1]) & (
        (cells % side)[None, :] < local_grids[:, 1:2]
    )
    image_allowed = jnp.broadcast_to(cell_valid[:, None, :], (images_here, cell_count, cell_count))
    residual, mine, other = layer(
        patches,
        image_allowed,
        encoder_attend_in,
        encoder_attend_out,
        encoder_expand,
        encoder_contract,
        encoder_gain_first,
        encoder_gain_second,
        split=True,
    )
    merged = merge(residual, mine, other, merge_weight)

    arrived = []
    for j in range(images_here):
        halves = []
        for flip in (0, 1):
            perm = [
                (r * 2 + t, (r ^ REQ_XOR[j]) * 2 + (t ^ flip))
                for r in range(req_count)
                for t in range(2)
            ]
            halves.append(lax.ppermute(merged[j], ("req", "tensor"), perm))
        same, other = halves
        low = jnp.where(core == 0, same, other)
        high = jnp.where(core == 0, other, same)
        arrived.append(jnp.concatenate([low, high], axis=-1))
    sources = [(device ^ REQ_XOR[j]) * images_here + j for j in range(images_here)]
    first_slot = place[sources[0]] % 2
    swap = first_slot != 0
    image_rows = jnp.where(
        swap,
        jnp.concatenate([arrived[1], arrived[0]], axis=0),
        jnp.concatenate([arrived[0], arrived[1]], axis=0),
    )
    grid_a = grids[sources[0]]
    grid_b = grids[sources[1]]
    slot_grids = jnp.where(swap, jnp.stack([grid_b, grid_a]), jnp.stack([grid_a, grid_b]))
    slots = jnp.arange(slot_count)
    merged_valid = ((2 * (slots // half))[None, :] < slot_grids[:, 0:1]) & (
        (2 * (slots % half))[None, :] < slot_grids[:, 1:2]
    )
    prompt = jnp.concatenate([image_rows, text_tokens[0]], axis=0)[None]
    text_count = text_tokens.shape[1]
    prompt_valid = jnp.concatenate(
        [merged_valid.reshape(-1), jnp.ones((text_count,), bool)], axis=0
    )
    length = prompt.shape[1]
    positions = jnp.arange(length)
    prompt_allowed = (prompt_valid[None, :] & (positions[None, :] <= positions[:, None]))[None]
    decoded = layer(
        prompt,
        prompt_allowed,
        decoder_attend_in,
        decoder_attend_out,
        decoder_expand,
        decoder_contract,
        decoder_gain_first,
        decoder_gain_second,
    )
    return jnp.where(prompt_valid[None, :, None], decoded, jnp.zeros_like(decoded))


def solution(mesh):
    placed = (
        P("req", None, None),
        P(),
        P(),
        P("req", None, None),
        P(None, None, "tensor"),
        P("tensor", None),
        P(None, "tensor"),
        P("tensor", None),
        P(),
        P(),
        P(None, "tensor"),
        P(None, None, "tensor"),
        P("tensor", None),
        P(None, "tensor"),
        P("tensor", None),
        P(),
        P(),
    )

    def body(*args):
        return on_device(mesh.shape["req"], *args)

    return jax.shard_map(
        body, mesh=mesh, in_specs=placed, out_specs=P("req", None, None), check_vma=False
    )
```

```python
import functools

import jax
import jax.numpy as jnp
from jax import lax
from jax.experimental import pallas as pl
from jax.experimental.pallas import tpu as pltpu
from jax.sharding import PartitionSpec as P

HEAD_DIM = 80
GRID = 16
REQ_XOR = (1, 64)


def normalize(values, gain):
    center = values - jnp.mean(values, axis=-1, keepdims=True)
    spread = jnp.mean(center * center, axis=-1, keepdims=True)
    return center * lax.rsqrt(spread + 1e-06) * gain


def tensor_sum(partial):
    mine = partial.astype(jnp.bfloat16)
    other = lax.ppermute(mine, "tensor", [(0, 1), (1, 0)])
    return mine.astype(jnp.float32) + other.astype(jnp.float32)


def _feed_forward_kernel(rows_per_step, x_ref, w1_ref, w2_ref, o_ref, acc_ref):
    k = pl.program_id(0)

    @pl.when(k == 0)
    def _():
        acc_ref[...] = jnp.zeros_like(acc_ref)

    w1 = w1_ref[...]
    w2 = w2_ref[...]
    for r in range(x_ref.shape[0] // rows_per_step):
        rows = pl.ds(r * rows_per_step, rows_per_step)
        h = jnp.dot(x_ref[rows, :], w1, preferred_element_type=jnp.float32)
        g = (h * 0.5 * (1.0 + lax.erf(h * (2.0 ** -0.5)))).astype(jnp.bfloat16)
        acc_ref[rows, :] += jnp.dot(g, w2, preferred_element_type=jnp.float32)

    @pl.when(k == pl.num_programs(0) - 1)
    def _():
        o_ref[...] = acc_ref[...].astype(o_ref.dtype)


def feed_forward(x, expand, contract, hidden_step=512, rows_per_step=128):
    length, width = x.shape
    hidden = expand.shape[1]
    return pl.pallas_call(
        functools.partial(_feed_forward_kernel, rows_per_step),
        out_shape=jax.ShapeDtypeStruct((length, width), jnp.bfloat16),
        grid=(hidden // hidden_step,),
        in_specs=[
            pl.BlockSpec((length, width), lambda k: (0, 0)),
            pl.BlockSpec((width, hidden_step), lambda k: (0, k)),
            pl.BlockSpec((hidden_step, width), lambda k: (k, 0)),
        ],
        out_specs=pl.BlockSpec((length, width), lambda k: (0, 0)),
        scratch_shapes=[pltpu.VMEM((length, width), jnp.float32)],
        cost_estimate=pl.CostEstimate(
            flops=4 * length * width * hidden,
            transcendentals=length * hidden,
            bytes_accessed=2 * (2 * width * hidden + 2 * length * width),
        ),
    )(x, expand, contract)


def _merge_kernel(res_ref, mine_ref, other_ref, w_ref, o_ref):
    cells, width = res_ref.shape[1], res_ref.shape[2]
    half = GRID // 2
    slot = lax.broadcasted_iota(jnp.int32, (half * half, cells), 0)
    cell = lax.broadcasted_iota(jnp.int32, (half * half, cells), 1)
    for i in range(res_ref.shape[0]):
        encoded = (
            res_ref[i] + (mine_ref[i].astype(jnp.float32) + other_ref[i].astype(jnp.float32))
        ).astype(jnp.bfloat16)
        total = None
        for a in range(2):
            for b in range(2):
                wanted = (2 * (slot // half) + a) * GRID + 2 * (slot % half) + b
                pick = jnp.where(cell == wanted, 1.0, 0.0).astype(jnp.bfloat16)
                rows = jnp.dot(pick, encoded, preferred_element_type=jnp.float32).astype(jnp.bfloat16)
                part = jnp.dot(
                    rows,
                    w_ref[pl.ds((2 * a + b) * width, width), :],
                    preferred_element_type=jnp.float32,
                )
                total = part if total is None else total + part
        o_ref[i] = total.astype(o_ref.dtype)


def merge(residual, mine, other, merge_weight):
    images, cells, width = residual.shape
    half = GRID // 2
    out_width = merge_weight.shape[1]
    return pl.pallas_call(
        _merge_kernel,
        out_shape=jax.ShapeDtypeStruct((images, half * half, out_width), jnp.bfloat16),
        cost_estimate=pl.CostEstimate(
            flops=2 * images * cells * width * (out_width + half * half),
            transcendentals=0,
            bytes_accessed=images * cells * width * 8 + merge_weight.size * 2,
        ),
    )(residual, mine, other, merge_weight)


def _attention_kernel(causal, q_ref, k_ref, v_ref, valid_ref, o_ref, acc_ref):
    length, width = q_ref.shape[2], q_ref.shape[3]
    window = 256
    keys = valid_ref[0] > 0
    if causal:
        row = lax.broadcasted_iota(jnp.int32, (length, length), 0)
        col = lax.broadcasted_iota(jnp.int32, (length, length), 1)
        allowed = keys & (col <= row)
    else:
        allowed = jnp.broadcast_to(keys, (length, length))
    acc_ref[...] = jnp.zeros_like(acc_ref)
    for h in range(width // HEAD_DIM):
        start = min((h * HEAD_DIM) // 128 * 128, width - window)
        lanes = pl.ds(start, window)
        lane = lax.broadcasted_iota(jnp.int32, (1, window), 1) + start
        mine = (lane >= h * HEAD_DIM) & (lane < (h + 1) * HEAD_DIM)
        zero = jnp.zeros((), q_ref.dtype)
        queries = jnp.where(mine, q_ref[0, 0, :, lanes], zero)
        scores = lax.dot_general(
            queries, k_ref[0, 0, :, lanes], (((1,), (1,)), ((), ())),
            preferred_element_type=jnp.float32,
        ) * HEAD_DIM ** (-0.5)
        scores = jnp.where(allowed, scores, jnp.float32(-1e30))
        top = jnp.max(scores, axis=-1, keepdims=True)
        raised = jnp.exp(scores - top)
        probs = (raised / jnp.sum(raised, axis=-1, keepdims=True)).astype(jnp.bfloat16)
        values = jnp.where(mine, v_ref[0, 0, :, lanes], zero)
        acc_ref[:, lanes] += jnp.dot(probs, values, preferred_element_type=jnp.float32)
    o_ref[0] = acc_ref[...].astype(o_ref.dtype)


def attend(projected, key_valid, causal, attend_out):
    batch, _, length, width = projected.shape
    part = lambda j: pl.BlockSpec((1, 1, length, width), lambda b: (b, j, 0, 0))
    mixed = pl.pallas_call(
        functools.partial(_attention_kernel, causal),
        out_shape=jax.ShapeDtypeStruct((batch, length, width), jnp.bfloat16),
        grid=(batch,),
        in_specs=[part(0), part(1), part(2), pl.BlockSpec((1, 1, length), lambda b: (b, 0, 0))],
        out_specs=pl.BlockSpec((1, length, width), lambda b: (b, 0, 0)),
        scratch_shapes=[pltpu.VMEM((length, width), jnp.float32)],
        cost_estimate=pl.CostEstimate(
            flops=4 * batch * length * length * 256 * (width // HEAD_DIM),
            transcendentals=batch * length * length * (width // HEAD_DIM),
            bytes_accessed=2 * 4 * batch * length * width,
        ),
    )(projected, projected, projected, key_valid.astype(jnp.int32).reshape(batch, 1, length))
    return jnp.dot(mixed, attend_out, preferred_element_type=jnp.float32)


def layer(inputs, key_valid, causal, attend_in, attend_out, expand, contract, gain_first, gain_second, split=False):
    widened = inputs.astype(jnp.float32)
    first = lax.optimization_barrier(normalize(widened, gain_first).astype(jnp.bfloat16))
    projected = jnp.einsum(
        "bld,dkf->bklf", first, attend_in, preferred_element_type=jnp.float32
    ).astype(jnp.bfloat16)
    attended = attend(projected, key_valid, causal, attend_out)
    residual = widened + tensor_sum(attended)
    second = normalize(residual, gain_second).astype(jnp.bfloat16)
    batch, length, width = second.shape
    partial_out = feed_forward(second.reshape(batch * length, width), expand, contract)
    mine = partial_out.reshape(batch, length, width)
    other = lax.ppermute(mine, "tensor", [(0, 1), (1, 0)])
    if split:
        return residual, mine, other
    return (residual + (mine.astype(jnp.float32) + other.astype(jnp.float32))).astype(jnp.bfloat16)


def on_device(
    req_count,
    patches,
    grids,
    place,
    text_tokens,
    encoder_attend_in,
    encoder_attend_out,
    encoder_expand,
    encoder_contract,
    encoder_gain_first,
    encoder_gain_second,
    merge_weight,
    decoder_attend_in,
    decoder_attend_out,
    decoder_expand,
    decoder_contract,
    decoder_gain_first,
    decoder_gain_second,
):
    device = lax.axis_index("req")
    core = lax.axis_index("tensor")
    images_here, cell_count, width = patches.shape
    side = GRID
    half = side // 2
    slot_count = half * half
    local_grids = lax.dynamic_slice_in_dim(grids, device * images_here, images_here, 0)
    cells = jnp.arange(cell_count)
    cell_valid = ((cells // side)[None, :] < local_grids[:, 0:1]) & (
        (cells % side)[None, :] < local_grids[:, 1:2]
    )
    residual, mine, other = layer(
        patches,
        cell_valid,
        False,
        encoder_attend_in,
        encoder_attend_out,
        encoder_expand,
        encoder_contract,
        encoder_gain_first,
        encoder_gain_second,
        split=True,
    )
    merged = merge(residual, mine, other, merge_weight)

    arrived = []
    for j in range(images_here):
        halves = []
        for flip in (0, 1):
            perm = [
                (r * 2 + t, (r ^ REQ_XOR[j]) * 2 + (t ^ flip))
                for r in range(req_count)
                for t in range(2)
            ]
            halves.append(lax.ppermute(merged[j], ("req", "tensor"), perm))
        same, other = halves
        low = jnp.where(core == 0, same, other)
        high = jnp.where(core == 0, other, same)
        arrived.append(jnp.concatenate([low, high], axis=-1))
    sources = [(device ^ REQ_XOR[j]) * images_here + j for j in range(images_here)]
    first_slot = place[sources[0]] % 2
    swap = first_slot != 0
    image_rows = jnp.where(
        swap,
        jnp.concatenate([arrived[1], arrived[0]], axis=0),
        jnp.concatenate([arrived[0], arrived[1]], axis=0),
    )
    grid_a = grids[sources[0]]
    grid_b = grids[sources[1]]
    slot_grids = jnp.where(swap, jnp.stack([grid_b, grid_a]), jnp.stack([grid_a, grid_b]))
    slots = jnp.arange(slot_count)
    merged_valid = ((2 * (slots // half))[None, :] < slot_grids[:, 0:1]) & (
        (2 * (slots % half))[None, :] < slot_grids[:, 1:2]
    )
    prompt = jnp.concatenate([image_rows, text_tokens[0]], axis=0)[None]
    text_count = text_tokens.shape[1]
    prompt_valid = jnp.concatenate(
        [merged_valid.reshape(-1), jnp.ones((text_count,), bool)], axis=0
    )
    decoded = layer(
        prompt,
        prompt_valid[None],
        True,
        decoder_attend_in,
        decoder_attend_out,
        decoder_expand,
        decoder_contract,
        decoder_gain_first,
        decoder_gain_second,
    )
    return jnp.where(prompt_valid[None, :, None], decoded, jnp.zeros_like(decoded))


def solution(mesh):
    placed = (
        P("req", None, None),
        P(),
        P(),
        P("req", None, None),
        P(None, None, "tensor"),
        P("tensor", None),
        P(None, "tensor"),
        P("tensor", None),
        P(),
        P(),
        P(None, "tensor"),
        P(None, None, "tensor"),
        P("tensor", None),
        P(None, "tensor"),
        P("tensor", None),
        P(),
        P(),
    )

    def body(*args):
        return on_device(mesh.shape["req"], *args)

    return jax.shard_map(
        body, mesh=mesh, in_specs=placed, out_specs=P("req", None, None), check_vma=False
    )
```

```python
import functools

import jax
import jax.numpy as jnp
from jax import lax
from jax.experimental import pallas as pl
from jax.experimental.pallas import tpu as pltpu
from jax.sharding import PartitionSpec as P

HEAD_DIM = 80
GRID = 16
REQ_XOR = (1, 64)


def normalize(values, gain):
    center = values - jnp.mean(values, axis=-1, keepdims=True)
    spread = jnp.mean(center * center, axis=-1, keepdims=True)
    return center * lax.rsqrt(spread + 1e-06) * gain


def tensor_sum(partial):
    mine = partial.astype(jnp.bfloat16)
    other = lax.ppermute(mine, "tensor", [(0, 1), (1, 0)])
    return mine.astype(jnp.float32) + other.astype(jnp.float32)


def _feed_forward_kernel(rows_per_step, x_ref, w1_ref, w2_ref, o_ref, acc_ref):
    k = pl.program_id(0)

    @pl.when(k == 0)
    def _():
        acc_ref[...] = jnp.zeros_like(acc_ref)

    w1 = w1_ref[...]
    w2 = w2_ref[...]
    for r in range(x_ref.shape[0] // rows_per_step):
        rows = pl.ds(r * rows_per_step, rows_per_step)
        h = jnp.dot(x_ref[rows, :], w1, preferred_element_type=jnp.float32)
        g = (h * 0.5 * (1.0 + lax.erf(h * (2.0 ** -0.5)))).astype(jnp.bfloat16)
        acc_ref[rows, :] += jnp.dot(g, w2, preferred_element_type=jnp.float32)

    @pl.when(k == pl.num_programs(0) - 1)
    def _():
        o_ref[...] = acc_ref[...].astype(o_ref.dtype)


def feed_forward(x, expand, contract, hidden_step=512, rows_per_step=128):
    length, width = x.shape
    hidden = expand.shape[1]
    return pl.pallas_call(
        functools.partial(_feed_forward_kernel, rows_per_step),
        out_shape=jax.ShapeDtypeStruct((length, width), jnp.bfloat16),
        grid=(hidden // hidden_step,),
        in_specs=[
            pl.BlockSpec((length, width), lambda k: (0, 0)),
            pl.BlockSpec((width, hidden_step), lambda k: (0, k)),
            pl.BlockSpec((hidden_step, width), lambda k: (k, 0)),
        ],
        out_specs=pl.BlockSpec((length, width), lambda k: (0, 0)),
        scratch_shapes=[pltpu.VMEM((length, width), jnp.float32)],
        cost_estimate=pl.CostEstimate(
            flops=4 * length * width * hidden,
            transcendentals=length * hidden,
            bytes_accessed=2 * (2 * width * hidden + 2 * length * width),
        ),
    )(x, expand, contract)


def _merge_kernel(res_ref, mine_ref, other_ref, w_ref, o_ref):
    cells, width = res_ref.shape[1], res_ref.shape[2]
    half = GRID // 2
    slot = lax.broadcasted_iota(jnp.int32, (half * half, cells), 0)
    cell = lax.broadcasted_iota(jnp.int32, (half * half, cells), 1)
    for i in range(res_ref.shape[0]):
        encoded = (
            res_ref[i] + (mine_ref[i].astype(jnp.float32) + other_ref[i].astype(jnp.float32))
        ).astype(jnp.bfloat16)
        total = None
        for a in range(2):
            for b in range(2):
                wanted = (2 * (slot // half) + a) * GRID + 2 * (slot % half) + b
                pick = jnp.where(cell == wanted, 1.0, 0.0).astype(jnp.bfloat16)
                rows = jnp.dot(pick, encoded, preferred_element_type=jnp.float32).astype(jnp.bfloat16)
                part = jnp.dot(
                    rows,
                    w_ref[pl.ds((2 * a + b) * width, width), :],
                    preferred_element_type=jnp.float32,
                )
                total = part if total is None else total + part
        o_ref[i] = total.astype(o_ref.dtype)


def merge(residual, mine, other, merge_weight):
    images, cells, width = residual.shape
    half = GRID // 2
    out_width = merge_weight.shape[1]
    return pl.pallas_call(
        _merge_kernel,
        out_shape=jax.ShapeDtypeStruct((images, half * half, out_width), jnp.bfloat16),
        cost_estimate=pl.CostEstimate(
            flops=2 * images * cells * width * (out_width + half * half),
            transcendentals=0,
            bytes_accessed=images * cells * width * 8 + merge_weight.size * 2,
        ),
    )(residual, mine, other, merge_weight)


def _attention_kernel(causal, x_ref, gain_ref, w_ref, valid_ref, o_ref, q_ref, k_ref, v_ref, acc_ref):
    length, width = q_ref.shape
    window = 256
    values = x_ref[0].astype(jnp.float32)
    center = values - jnp.mean(values, axis=-1, keepdims=True)
    spread = jnp.mean(center * center, axis=-1, keepdims=True)
    first = (center * lax.rsqrt(spread + 1e-06) * gain_ref[...]).astype(jnp.bfloat16)
    for j, ref in enumerate((q_ref, k_ref, v_ref)):
        ref[...] = jnp.dot(first, w_ref[j], preferred_element_type=jnp.float32).astype(ref.dtype)
    keys = valid_ref[0] > 0
    if causal:
        row = lax.broadcasted_iota(jnp.int32, (length, length), 0)
        col = lax.broadcasted_iota(jnp.int32, (length, length), 1)
        allowed = keys & (col <= row)
    else:
        allowed = jnp.broadcast_to(keys, (length, length))
    acc_ref[...] = jnp.zeros_like(acc_ref)
    for h in range(width // HEAD_DIM):
        start = min((h * HEAD_DIM) // 128 * 128, width - window)
        lanes = pl.ds(start, window)
        lane = lax.broadcasted_iota(jnp.int32, (1, window), 1) + start
        mine = (lane >= h * HEAD_DIM) & (lane < (h + 1) * HEAD_DIM)
        zero = jnp.zeros((), q_ref.dtype)
        queries = jnp.where(mine, q_ref[:, lanes], zero)
        scores = lax.dot_general(
            queries, k_ref[:, lanes], (((1,), (1,)), ((), ())),
            preferred_element_type=jnp.float32,
        ) * HEAD_DIM ** (-0.5)
        scores = jnp.where(allowed, scores, jnp.float32(-1e30))
        top = jnp.max(scores, axis=-1, keepdims=True)
        raised = jnp.exp(scores - top)
        probs = (raised / jnp.sum(raised, axis=-1, keepdims=True)).astype(jnp.bfloat16)
        values_h = jnp.where(mine, v_ref[:, lanes], zero)
        acc_ref[:, lanes] += jnp.dot(probs, values_h, preferred_element_type=jnp.float32)
    o_ref[0] = acc_ref[...].astype(o_ref.dtype)


def attend(inputs, gain_first, attend_in, key_valid, causal, attend_out):
    batch, length, model_width = inputs.shape
    width = attend_in.shape[2]
    weight = jnp.transpose(attend_in, (1, 0, 2))
    mixed = pl.pallas_call(
        functools.partial(_attention_kernel, causal),
        out_shape=jax.ShapeDtypeStruct((batch, length, width), jnp.bfloat16),
        grid=(batch,),
        in_specs=[
            pl.BlockSpec((1, length, model_width), lambda b: (b, 0, 0)),
            pl.BlockSpec((1, model_width), lambda b: (0, 0)),
            pl.BlockSpec((3, model_width, width), lambda b: (0, 0, 0)),
            pl.BlockSpec((1, 1, length), lambda b: (b, 0, 0)),
        ],
        out_specs=pl.BlockSpec((1, length, width), lambda b: (b, 0, 0)),
        scratch_shapes=[pltpu.VMEM((length, width), jnp.bfloat16)] * 3
        + [pltpu.VMEM((length, width), jnp.float32)],
        cost_estimate=pl.CostEstimate(
            flops=batch * length * (6 * model_width * width + 4 * length * 256 * (width // HEAD_DIM)),
            transcendentals=batch * length * length * (width // HEAD_DIM),
            bytes_accessed=2 * (batch * length * (model_width + width) + 3 * model_width * width),
        ),
    )(
        inputs,
        gain_first.reshape(1, model_width),
        weight,
        key_valid.astype(jnp.int32).reshape(batch, 1, length),
    )
    return jnp.dot(mixed, attend_out, preferred_element_type=jnp.float32)


def layer(inputs, key_valid, causal, attend_in, attend_out, expand, contract, gain_first, gain_second, split=False):
    widened = inputs.astype(jnp.float32)
    attended = attend(inputs, gain_first, attend_in, key_valid, causal, attend_out)
    residual = widened + tensor_sum(attended)
    second = normalize(residual, gain_second).astype(jnp.bfloat16)
    batch, length, width = second.shape
    partial_out = feed_forward(second.reshape(batch * length, width), expand, contract)
    mine = partial_out.reshape(batch, length, width)
    other = lax.ppermute(mine, "tensor", [(0, 1), (1, 0)])
    if split:
        return residual, mine, other
    return (residual + (mine.astype(jnp.float32) + other.astype(jnp.float32))).astype(jnp.bfloat16)


def on_device(
    req_count,
    patches,
    grids,
    place,
    text_tokens,
    encoder_attend_in,
    encoder_attend_out,
    encoder_expand,
    encoder_contract,
    encoder_gain_first,
    encoder_gain_second,
    merge_weight,
    decoder_attend_in,
    decoder_attend_out,
    decoder_expand,
    decoder_contract,
    decoder_gain_first,
    decoder_gain_second,
):
    device = lax.axis_index("req")
    core = lax.axis_index("tensor")
    images_here, cell_count, width = patches.shape
    side = GRID
    half = side // 2
    slot_count = half * half
    local_grids = lax.dynamic_slice_in_dim(grids, device * images_here, images_here, 0)
    cells = jnp.arange(cell_count)
    cell_valid = ((cells // side)[None, :] < local_grids[:, 0:1]) & (
        (cells % side)[None, :] < local_grids[:, 1:2]
    )
    residual, mine, other = layer(
        patches,
        cell_valid,
        False,
        encoder_attend_in,
        encoder_attend_out,
        encoder_expand,
        encoder_contract,
        encoder_gain_first,
        encoder_gain_second,
        split=True,
    )
    merged = merge(residual, mine, other, merge_weight)

    arrived = []
    for j in range(images_here):
        halves = []
        for flip in (0, 1):
            perm = [
                (r * 2 + t, (r ^ REQ_XOR[j]) * 2 + (t ^ flip))
                for r in range(req_count)
                for t in range(2)
            ]
            halves.append(lax.ppermute(merged[j], ("req", "tensor"), perm))
        same, other = halves
        low = jnp.where(core == 0, same, other)
        high = jnp.where(core == 0, other, same)
        arrived.append(jnp.concatenate([low, high], axis=-1))
    sources = [(device ^ REQ_XOR[j]) * images_here + j for j in range(images_here)]
    first_slot = place[sources[0]] % 2
    swap = first_slot != 0
    image_rows = jnp.where(
        swap,
        jnp.concatenate([arrived[1], arrived[0]], axis=0),
        jnp.concatenate([arrived[0], arrived[1]], axis=0),
    )
    grid_a = grids[sources[0]]
    grid_b = grids[sources[1]]
    slot_grids = jnp.where(swap, jnp.stack([grid_b, grid_a]), jnp.stack([grid_a, grid_b]))
    slots = jnp.arange(slot_count)
    merged_valid = ((2 * (slots // half))[None, :] < slot_grids[:, 0:1]) & (
        (2 * (slots % half))[None, :] < slot_grids[:, 1:2]
    )
    prompt = jnp.concatenate([image_rows, text_tokens[0]], axis=0)[None]
    text_count = text_tokens.shape[1]
    prompt_valid = jnp.concatenate(
        [merged_valid.reshape(-1), jnp.ones((text_count,), bool)], axis=0
    )
    decoded = layer(
        prompt,
        prompt_valid[None],
        True,
        decoder_attend_in,
        decoder_attend_out,
        decoder_expand,
        decoder_contract,
        decoder_gain_first,
        decoder_gain_second,
    )
    return jnp.where(prompt_valid[None, :, None], decoded, jnp.zeros_like(decoded))


def solution(mesh):
    placed = (
        P("req", None, None),
        P(),
        P(),
        P("req", None, None),
        P(None, None, "tensor"),
        P("tensor", None),
        P(None, "tensor"),
        P("tensor", None),
        P(),
        P(),
        P(None, "tensor"),
        P(None, None, "tensor"),
        P("tensor", None),
        P(None, "tensor"),
        P("tensor", None),
        P(),
        P(),
    )

    def body(*args):
        return on_device(mesh.shape["req"], *args)

    return jax.shard_map(
        body, mesh=mesh, in_specs=placed, out_specs=P("req", None, None), check_vma=False
    )
```

```python
import functools

import jax
import jax.numpy as jnp
from jax import lax
from jax.experimental import pallas as pl
from jax.experimental.pallas import tpu as pltpu
from jax.sharding import PartitionSpec as P

HEAD_DIM = 80
GRID = 16
REQ_XOR = (1, 64)


def normalize(values, gain):
    center = values - jnp.mean(values, axis=-1, keepdims=True)
    spread = jnp.mean(center * center, axis=-1, keepdims=True)
    return center * lax.rsqrt(spread + 1e-06) * gain


def tensor_sum(partial):
    mine = partial.astype(jnp.bfloat16)
    other = lax.ppermute(mine, "tensor", [(0, 1), (1, 0)])
    return mine.astype(jnp.float32) + other.astype(jnp.float32)


def _feed_forward_kernel(rows_per_step, x_ref, w1_ref, w2_ref, o_ref, acc_ref):
    k = pl.program_id(0)

    @pl.when(k == 0)
    def _():
        acc_ref[...] = jnp.zeros_like(acc_ref)

    w1 = w1_ref[...]
    w2 = w2_ref[...]
    for r in range(x_ref.shape[0] // rows_per_step):
        rows = pl.ds(r * rows_per_step, rows_per_step)
        h = jnp.dot(x_ref[rows, :], w1, preferred_element_type=jnp.float32)
        g = (h * 0.5 * (1.0 + lax.erf(h * (2.0 ** -0.5)))).astype(jnp.bfloat16)
        acc_ref[rows, :] += jnp.dot(g, w2, preferred_element_type=jnp.float32)

    @pl.when(k == pl.num_programs(0) - 1)
    def _():
        o_ref[...] = acc_ref[...].astype(o_ref.dtype)


def feed_forward(x, expand, contract, hidden_step=512, rows_per_step=256):
    length, width = x.shape
    hidden = expand.shape[1]
    return pl.pallas_call(
        functools.partial(_feed_forward_kernel, rows_per_step),
        out_shape=jax.ShapeDtypeStruct((length, width), jnp.bfloat16),
        grid=(hidden // hidden_step,),
        in_specs=[
            pl.BlockSpec((length, width), lambda k: (0, 0)),
            pl.BlockSpec((width, hidden_step), lambda k: (0, k)),
            pl.BlockSpec((hidden_step, width), lambda k: (k, 0)),
        ],
        out_specs=pl.BlockSpec((length, width), lambda k: (0, 0)),
        scratch_shapes=[pltpu.VMEM((length, width), jnp.float32)],
        cost_estimate=pl.CostEstimate(
            flops=4 * length * width * hidden,
            transcendentals=length * hidden,
            bytes_accessed=2 * (2 * width * hidden + 2 * length * width),
        ),
    )(x, expand, contract)


def _merge_kernel(res_ref, mine_ref, other_ref, w_ref, o_ref):
    cells, width = res_ref.shape[1], res_ref.shape[2]
    half = GRID // 2
    slot = lax.broadcasted_iota(jnp.int32, (half * half, cells), 0)
    cell = lax.broadcasted_iota(jnp.int32, (half * half, cells), 1)
    for i in range(res_ref.shape[0]):
        encoded = (
            res_ref[i] + (mine_ref[i].astype(jnp.float32) + other_ref[i].astype(jnp.float32))
        ).astype(jnp.bfloat16)
        total = None
        for a in range(2):
            for b in range(2):
                wanted = (2 * (slot // half) + a) * GRID + 2 * (slot % half) + b
                pick = jnp.where(cell == wanted, 1.0, 0.0).astype(jnp.bfloat16)
                rows = jnp.dot(pick, encoded, preferred_element_type=jnp.float32).astype(jnp.bfloat16)
                part = jnp.dot(
                    rows,
                    w_ref[pl.ds((2 * a + b) * width, width), :],
                    preferred_element_type=jnp.float32,
                )
                total = part if total is None else total + part
        o_ref[i] = total.astype(o_ref.dtype)


def merge(residual, mine, other, merge_weight):
    images, cells, width = residual.shape
    half = GRID // 2
    out_width = merge_weight.shape[1]
    return pl.pallas_call(
        _merge_kernel,
        out_shape=jax.ShapeDtypeStruct((images, half * half, out_width), jnp.bfloat16),
        cost_estimate=pl.CostEstimate(
            flops=2 * images * cells * width * (out_width + half * half),
            transcendentals=0,
            bytes_accessed=images * cells * width * 8 + merge_weight.size * 2,
        ),
    )(residual, mine, other, merge_weight)


def _attention_kernel(causal, x_ref, gain_ref, w_ref, valid_ref, wo_ref, o_ref, q_ref, k_ref, v_ref, acc_ref):
    length, width = q_ref.shape
    window = 256
    values = x_ref[0].astype(jnp.float32)
    center = values - jnp.mean(values, axis=-1, keepdims=True)
    spread = jnp.mean(center * center, axis=-1, keepdims=True)
    first = (center * lax.rsqrt(spread + 1e-06) * gain_ref[...]).astype(jnp.bfloat16)
    for j, ref in enumerate((q_ref, k_ref, v_ref)):
        ref[...] = jnp.dot(first, w_ref[j], preferred_element_type=jnp.float32).astype(ref.dtype)
    keys = valid_ref[0] > 0
    if causal:
        row = lax.broadcasted_iota(jnp.int32, (length, length), 0)
        col = lax.broadcasted_iota(jnp.int32, (length, length), 1)
        allowed = keys & (col <= row)
    else:
        allowed = jnp.broadcast_to(keys, (length, length))
    acc_ref[...] = jnp.zeros_like(acc_ref)
    for h in range(width // HEAD_DIM):
        start = min((h * HEAD_DIM) // 128 * 128, width - window)
        lanes = pl.ds(start, window)
        lane = lax.broadcasted_iota(jnp.int32, (1, window), 1) + start
        mine = (lane >= h * HEAD_DIM) & (lane < (h + 1) * HEAD_DIM)
        zero = jnp.zeros((), q_ref.dtype)
        queries = jnp.where(mine, q_ref[:, lanes], zero)
        scores = lax.dot_general(
            queries, k_ref[:, lanes], (((1,), (1,)), ((), ())),
            preferred_element_type=jnp.float32,
        ) * HEAD_DIM ** (-0.5)
        scores = jnp.where(allowed, scores, jnp.float32(-1e30))
        top = jnp.max(scores, axis=-1, keepdims=True)
        raised = jnp.exp(scores - top)
        probs = (raised / jnp.sum(raised, axis=-1, keepdims=True)).astype(jnp.bfloat16)
        values_h = jnp.where(mine, v_ref[:, lanes], zero)
        acc_ref[:, lanes] += jnp.dot(probs, values_h, preferred_element_type=jnp.float32)
    mixed = acc_ref[...].astype(jnp.bfloat16)
    o_ref[0] = jnp.dot(mixed, wo_ref[...], preferred_element_type=jnp.float32).astype(o_ref.dtype)


def attend(inputs, gain_first, attend_in, key_valid, causal, attend_out):
    batch, length, model_width = inputs.shape
    width = attend_in.shape[2]
    weight = jnp.transpose(attend_in, (1, 0, 2))
    mixed = pl.pallas_call(
        functools.partial(_attention_kernel, causal),
        out_shape=jax.ShapeDtypeStruct((batch, length, model_width), jnp.bfloat16),
        grid=(batch,),
        in_specs=[
            pl.BlockSpec((1, length, model_width), lambda b: (b, 0, 0)),
            pl.BlockSpec((1, model_width), lambda b: (0, 0)),
            pl.BlockSpec((3, model_width, width), lambda b: (0, 0, 0)),
            pl.BlockSpec((1, 1, length), lambda b: (b, 0, 0)),
            pl.BlockSpec((width, model_width), lambda b: (0, 0)),
        ],
        out_specs=pl.BlockSpec((1, length, model_width), lambda b: (b, 0, 0)),
        scratch_shapes=[pltpu.VMEM((length, width), jnp.bfloat16)] * 3
        + [pltpu.VMEM((length, width), jnp.float32)],
        cost_estimate=pl.CostEstimate(
            flops=batch * length * (8 * model_width * width + 4 * length * 256 * (width // HEAD_DIM)),
            transcendentals=batch * length * length * (width // HEAD_DIM),
            bytes_accessed=2 * (2 * batch * length * model_width + 4 * model_width * width),
        ),
    )(
        inputs,
        gain_first.reshape(1, model_width),
        weight,
        key_valid.astype(jnp.int32).reshape(batch, 1, length),
        attend_out,
    )
    return mixed


def layer(inputs, key_valid, causal, attend_in, attend_out, expand, contract, gain_first, gain_second, split=False):
    widened = inputs.astype(jnp.float32)
    attended = attend(inputs, gain_first, attend_in, key_valid, causal, attend_out)
    residual = widened + tensor_sum(attended)
    second = normalize(residual, gain_second).astype(jnp.bfloat16)
    batch, length, width = second.shape
    partial_out = feed_forward(second.reshape(batch * length, width), expand, contract)
    mine = partial_out.reshape(batch, length, width)
    other = lax.ppermute(mine, "tensor", [(0, 1), (1, 0)])
    if split:
        return residual, mine, other
    return (residual + (mine.astype(jnp.float32) + other.astype(jnp.float32))).astype(jnp.bfloat16)


def on_device(
    req_count,
    patches,
    grids,
    place,
    text_tokens,
    encoder_attend_in,
    encoder_attend_out,
    encoder_expand,
    encoder_contract,
    encoder_gain_first,
    encoder_gain_second,
    merge_weight,
    decoder_attend_in,
    decoder_attend_out,
    decoder_expand,
    decoder_contract,
    decoder_gain_first,
    decoder_gain_second,
):
    device = lax.axis_index("req")
    core = lax.axis_index("tensor")
    images_here, cell_count, width = patches.shape
    side = GRID
    half = side // 2
    slot_count = half * half
    local_grids = lax.dynamic_slice_in_dim(grids, device * images_here, images_here, 0)
    cells = jnp.arange(cell_count)
    cell_valid = ((cells // side)[None, :] < local_grids[:, 0:1]) & (
        (cells % side)[None, :] < local_grids[:, 1:2]
    )
    residual, mine, other = layer(
        patches,
        cell_valid,
        False,
        encoder_attend_in,
        encoder_attend_out,
        encoder_expand,
        encoder_contract,
        encoder_gain_first,
        encoder_gain_second,
        split=True,
    )
    merged = merge(residual, mine, other, merge_weight)

    arrived = []
    for j in range(images_here):
        halves = []
        for flip in (0, 1):
            perm = [
                (r * 2 + t, (r ^ REQ_XOR[j]) * 2 + (t ^ flip))
                for r in range(req_count)
                for t in range(2)
            ]
            halves.append(lax.ppermute(merged[j], ("req", "tensor"), perm))
        same, other = halves
        low = jnp.where(core == 0, same, other)
        high = jnp.where(core == 0, other, same)
        arrived.append(jnp.concatenate([low, high], axis=-1))
    sources = [(device ^ REQ_XOR[j]) * images_here + j for j in range(images_here)]
    first_slot = place[sources[0]] % 2
    swap = first_slot != 0
    image_rows = jnp.where(
        swap,
        jnp.concatenate([arrived[1], arrived[0]], axis=0),
        jnp.concatenate([arrived[0], arrived[1]], axis=0),
    )
    grid_a = grids[sources[0]]
    grid_b = grids[sources[1]]
    slot_grids = jnp.where(swap, jnp.stack([grid_b, grid_a]), jnp.stack([grid_a, grid_b]))
    slots = jnp.arange(slot_count)
    merged_valid = ((2 * (slots // half))[None, :] < slot_grids[:, 0:1]) & (
        (2 * (slots % half))[None, :] < slot_grids[:, 1:2]
    )
    prompt = jnp.concatenate([image_rows, text_tokens[0]], axis=0)[None]
    text_count = text_tokens.shape[1]
    prompt_valid = jnp.concatenate(
        [merged_valid.reshape(-1), jnp.ones((text_count,), bool)], axis=0
    )
    decoded = layer(
        prompt,
        prompt_valid[None],
        True,
        decoder_attend_in,
        decoder_attend_out,
        decoder_expand,
        decoder_contract,
        decoder_gain_first,
        decoder_gain_second,
    )
    return jnp.where(prompt_valid[None, :, None], decoded, jnp.zeros_like(decoded))


def solution(mesh):
    placed = (
        P("req", None, None),
        P(),
        P(),
        P("req", None, None),
        P(None, None, "tensor"),
        P("tensor", None),
        P(None, "tensor"),
        P("tensor", None),
        P(),
        P(),
        P(None, "tensor"),
        P(None, None, "tensor"),
        P("tensor", None),
        P(None, "tensor"),
        P("tensor", None),
        P(),
        P(),
    )

    def body(*args):
        return on_device(mesh.shape["req"], *args)

    return jax.shard_map(
        body, mesh=mesh, in_specs=placed, out_specs=P("req", None, None), check_vma=False
    )
```

```python
import functools

import jax
import jax.numpy as jnp
from jax import lax
from jax.experimental import pallas as pl
from jax.experimental.pallas import tpu as pltpu
from jax.sharding import PartitionSpec as P

HEAD_DIM = 80
GRID = 16
REQ_XOR = (1, 64)


def normalize(values, gain):
    center = values - jnp.mean(values, axis=-1, keepdims=True)
    spread = jnp.mean(center * center, axis=-1, keepdims=True)
    return center * lax.rsqrt(spread + 1e-06) * gain


def tensor_sum(partial):
    mine = partial.astype(jnp.bfloat16)
    other = lax.ppermute(mine, "tensor", [(0, 1), (1, 0)])
    return mine.astype(jnp.float32) + other.astype(jnp.float32)


def _feed_forward_kernel(rows_per_step, x_ref, w1_ref, w2_ref, o_ref, acc_ref):
    k = pl.program_id(0)

    @pl.when(k == 0)
    def _():
        acc_ref[...] = jnp.zeros_like(acc_ref)

    w1 = w1_ref[...]
    w2 = w2_ref[...]
    for r in range(x_ref.shape[0] // rows_per_step):
        rows = pl.ds(r * rows_per_step, rows_per_step)
        h = jnp.dot(x_ref[rows, :], w1, preferred_element_type=jnp.float32)
        g = (h * 0.5 * (1.0 + lax.erf(h * (2.0 ** -0.5)))).astype(jnp.bfloat16)
        acc_ref[rows, :] += jnp.dot(g, w2, preferred_element_type=jnp.float32)

    @pl.when(k == pl.num_programs(0) - 1)
    def _():
        o_ref[...] = acc_ref[...].astype(o_ref.dtype)


def feed_forward(x, expand, contract, hidden_step=512, rows_per_step=512):
    length, width = x.shape
    hidden = expand.shape[1]
    return pl.pallas_call(
        functools.partial(_feed_forward_kernel, rows_per_step),
        out_shape=jax.ShapeDtypeStruct((length, width), jnp.bfloat16),
        grid=(hidden // hidden_step,),
        in_specs=[
            pl.BlockSpec((length, width), lambda k: (0, 0)),
            pl.BlockSpec((width, hidden_step), lambda k: (0, k)),
            pl.BlockSpec((hidden_step, width), lambda k: (k, 0)),
        ],
        out_specs=pl.BlockSpec((length, width), lambda k: (0, 0)),
        scratch_shapes=[pltpu.VMEM((length, width), jnp.float32)],
        cost_estimate=pl.CostEstimate(
            flops=4 * length * width * hidden,
            transcendentals=length * hidden,
            bytes_accessed=2 * (2 * width * hidden + 2 * length * width),
        ),
    )(x, expand, contract)


def _merge_kernel(res_ref, mine_ref, other_ref, w_ref, o_ref):
    cells, width = res_ref.shape[1], res_ref.shape[2]
    half = GRID // 2
    slot = lax.broadcasted_iota(jnp.int32, (half * half, cells), 0)
    cell = lax.broadcasted_iota(jnp.int32, (half * half, cells), 1)
    for i in range(res_ref.shape[0]):
        encoded = (
            res_ref[i] + (mine_ref[i].astype(jnp.float32) + other_ref[i].astype(jnp.float32))
        ).astype(jnp.bfloat16)
        total = None
        for a in range(2):
            for b in range(2):
                wanted = (2 * (slot // half) + a) * GRID + 2 * (slot % half) + b
                pick = jnp.where(cell == wanted, 1.0, 0.0).astype(jnp.bfloat16)
                rows = jnp.dot(pick, encoded, preferred_element_type=jnp.float32).astype(jnp.bfloat16)
                part = jnp.dot(
                    rows,
                    w_ref[pl.ds((2 * a + b) * width, width), :],
                    preferred_element_type=jnp.float32,
                )
                total = part if total is None else total + part
        o_ref[i] = total.astype(o_ref.dtype)


def merge(residual, mine, other, merge_weight):
    images, cells, width = residual.shape
    half = GRID // 2
    out_width = merge_weight.shape[1]
    return pl.pallas_call(
        _merge_kernel,
        out_shape=jax.ShapeDtypeStruct((images, half * half, out_width), jnp.bfloat16),
        cost_estimate=pl.CostEstimate(
            flops=2 * images * cells * width * (out_width + half * half),
            transcendentals=0,
            bytes_accessed=images * cells * width * 8 + merge_weight.size * 2,
        ),
    )(residual, mine, other, merge_weight)


def _attention_kernel(causal, x_ref, gain_ref, w_ref, valid_ref, wo_ref, o_ref, q_ref, k_ref, v_ref, acc_ref):
    length, width = q_ref.shape
    window = 256
    values = x_ref[0].astype(jnp.float32)
    center = values - jnp.mean(values, axis=-1, keepdims=True)
    spread = jnp.mean(center * center, axis=-1, keepdims=True)
    first = (center * lax.rsqrt(spread + 1e-06) * gain_ref[...]).astype(jnp.bfloat16)
    for j, ref in enumerate((q_ref, k_ref, v_ref)):
        ref[...] = jnp.dot(first, w_ref[j], preferred_element_type=jnp.float32).astype(ref.dtype)
    keys = valid_ref[0] > 0
    if causal:
        row = lax.broadcasted_iota(jnp.int32, (length, length), 0)
        col = lax.broadcasted_iota(jnp.int32, (length, length), 1)
        allowed = keys & (col <= row)
    else:
        allowed = jnp.broadcast_to(keys, (length, length))
    acc_ref[...] = jnp.zeros_like(acc_ref)
    for h in range(width // HEAD_DIM):
        start = min((h * HEAD_DIM) // 128 * 128, width - window)
        lanes = pl.ds(start, window)
        lane = lax.broadcasted_iota(jnp.int32, (1, window), 1) + start
        mine = (lane >= h * HEAD_DIM) & (lane < (h + 1) * HEAD_DIM)
        zero = jnp.zeros((), q_ref.dtype)
        queries = jnp.where(mine, q_ref[:, lanes], zero)
        scores = lax.dot_general(
            queries, k_ref[:, lanes], (((1,), (1,)), ((), ())),
            preferred_element_type=jnp.float32,
        ) * HEAD_DIM ** (-0.5)
        scores = jnp.where(allowed, scores, jnp.float32(-1e30))
        top = jnp.max(scores, axis=-1, keepdims=True)
        raised = jnp.exp(scores - top)
        probs = (raised / jnp.sum(raised, axis=-1, keepdims=True)).astype(jnp.bfloat16)
        values_h = jnp.where(mine, v_ref[:, lanes], zero)
        acc_ref[:, lanes] += jnp.dot(probs, values_h, preferred_element_type=jnp.float32)
    mixed = acc_ref[...].astype(jnp.bfloat16)
    o_ref[0] = jnp.dot(mixed, wo_ref[...], preferred_element_type=jnp.float32).astype(o_ref.dtype)


def attend(inputs, gain_first, attend_in, key_valid, causal, attend_out):
    batch, length, model_width = inputs.shape
    width = attend_in.shape[2]
    weight = jnp.transpose(attend_in, (1, 0, 2))
    mixed = pl.pallas_call(
        functools.partial(_attention_kernel, causal),
        out_shape=jax.ShapeDtypeStruct((batch, length, model_width), jnp.bfloat16),
        grid=(batch,),
        in_specs=[
            pl.BlockSpec((1, length, model_width), lambda b: (b, 0, 0)),
            pl.BlockSpec((1, model_width), lambda b: (0, 0)),
            pl.BlockSpec((3, model_width, width), lambda b: (0, 0, 0)),
            pl.BlockSpec((1, 1, length), lambda b: (b, 0, 0)),
            pl.BlockSpec((width, model_width), lambda b: (0, 0)),
        ],
        out_specs=pl.BlockSpec((1, length, model_width), lambda b: (b, 0, 0)),
        scratch_shapes=[pltpu.VMEM((length, width), jnp.bfloat16)] * 3
        + [pltpu.VMEM((length, width), jnp.float32)],
        cost_estimate=pl.CostEstimate(
            flops=batch * length * (8 * model_width * width + 4 * length * 256 * (width // HEAD_DIM)),
            transcendentals=batch * length * length * (width // HEAD_DIM),
            bytes_accessed=2 * (2 * batch * length * model_width + 4 * model_width * width),
        ),
    )(
        inputs,
        gain_first.reshape(1, model_width),
        weight,
        key_valid.astype(jnp.int32).reshape(batch, 1, length),
        attend_out,
    )
    return mixed


def layer(inputs, key_valid, causal, attend_in, attend_out, expand, contract, gain_first, gain_second, split=False):
    widened = inputs.astype(jnp.float32)
    attended = attend(inputs, gain_first, attend_in, key_valid, causal, attend_out)
    residual = widened + tensor_sum(attended)
    second = normalize(residual, gain_second).astype(jnp.bfloat16)
    batch, length, width = second.shape
    partial_out = feed_forward(second.reshape(batch * length, width), expand, contract)
    mine = partial_out.reshape(batch, length, width)
    other = lax.ppermute(mine, "tensor", [(0, 1), (1, 0)])
    if split:
        return residual, mine, other
    return (residual + (mine.astype(jnp.float32) + other.astype(jnp.float32))).astype(jnp.bfloat16)


def on_device(
    req_count,
    patches,
    grids,
    place,
    text_tokens,
    encoder_attend_in,
    encoder_attend_out,
    encoder_expand,
    encoder_contract,
    encoder_gain_first,
    encoder_gain_second,
    merge_weight,
    decoder_attend_in,
    decoder_attend_out,
    decoder_expand,
    decoder_contract,
    decoder_gain_first,
    decoder_gain_second,
):
    device = lax.axis_index("req")
    core = lax.axis_index("tensor")
    images_here, cell_count, width = patches.shape
    side = GRID
    half = side // 2
    slot_count = half * half
    local_grids = lax.dynamic_slice_in_dim(grids, device * images_here, images_here, 0)
    cells = jnp.arange(cell_count)
    cell_valid = ((cells // side)[None, :] < local_grids[:, 0:1]) & (
        (cells % side)[None, :] < local_grids[:, 1:2]
    )
    residual, mine, other = layer(
        patches,
        cell_valid,
        False,
        encoder_attend_in,
        encoder_attend_out,
        encoder_expand,
        encoder_contract,
        encoder_gain_first,
        encoder_gain_second,
        split=True,
    )
    merged = merge(residual, mine, other, merge_weight)

    swap_pair = [(0, 1), (1, 0)]
    given = lax.ppermute(jnp.where(core == 0, merged[1], merged[0]), "tensor", swap_pair)
    own_image = jnp.where(
        core == 0,
        jnp.concatenate([merged[0], given], axis=-1),
        jnp.concatenate([given, merged[1]], axis=-1),
    )
    sent = []
    for flip in (0, 1):
        perm = [
            (r * 2 + t, (r ^ REQ_XOR[t]) * 2 + (t ^ flip))
            for r in range(req_count)
            for t in range(2)
        ]
        sent.append(lax.ppermute(own_image, ("req", "tensor"), perm))
    arrived = [
        jnp.where(core == 0, sent[0], sent[1]),
        jnp.where(core == 0, sent[1], sent[0]),
    ]
    sources = [(device ^ REQ_XOR[j]) * images_here + j for j in range(images_here)]
    first_slot = place[sources[0]] % 2
    swap = first_slot != 0
    image_rows = jnp.where(
        swap,
        jnp.concatenate([arrived[1], arrived[0]], axis=0),
        jnp.concatenate([arrived[0], arrived[1]], axis=0),
    )
    grid_a = grids[sources[0]]
    grid_b = grids[sources[1]]
    slot_grids = jnp.where(swap, jnp.stack([grid_b, grid_a]), jnp.stack([grid_a, grid_b]))
    slots = jnp.arange(slot_count)
    merged_valid = ((2 * (slots // half))[None, :] < slot_grids[:, 0:1]) & (
        (2 * (slots % half))[None, :] < slot_grids[:, 1:2]
    )
    prompt = jnp.concatenate([image_rows, text_tokens[0]], axis=0)[None]
    text_count = text_tokens.shape[1]
    prompt_valid = jnp.concatenate(
        [merged_valid.reshape(-1), jnp.ones((text_count,), bool)], axis=0
    )
    decoded = layer(
        prompt,
        prompt_valid[None],
        True,
        decoder_attend_in,
        decoder_attend_out,
        decoder_expand,
        decoder_contract,
        decoder_gain_first,
        decoder_gain_second,
    )
    return jnp.where(prompt_valid[None, :, None], decoded, jnp.zeros_like(decoded))


def solution(mesh):
    placed = (
        P("req", None, None),
        P(),
        P(),
        P("req", None, None),
        P(None, None, "tensor"),
        P("tensor", None),
        P(None, "tensor"),
        P("tensor", None),
        P(),
        P(),
        P(None, "tensor"),
        P(None, None, "tensor"),
        P("tensor", None),
        P(None, "tensor"),
        P("tensor", None),
        P(),
        P(),
    )

    def body(*args):
        return on_device(mesh.shape["req"], *args)

    return jax.shard_map(
        body, mesh=mesh, in_specs=placed, out_specs=P("req", None, None), check_vma=False
    )
```

```python
import functools

import jax
import jax.numpy as jnp
from jax import lax
from jax.experimental import pallas as pl
from jax.experimental.pallas import tpu as pltpu
from jax.sharding import PartitionSpec as P

HEAD_DIM = 80
GRID = 16
REQ_XOR = (1, 64)


def normalize(values, gain):
    center = values - jnp.mean(values, axis=-1, keepdims=True)
    spread = jnp.mean(center * center, axis=-1, keepdims=True)
    return center * lax.rsqrt(spread + 1e-06) * gain


def tensor_sum(partial):
    mine = partial.astype(jnp.bfloat16)
    other = lax.ppermute(mine, "tensor", [(0, 1), (1, 0)])
    return mine.astype(jnp.float32) + other.astype(jnp.float32)


def _feed_forward_kernel(rows_per_step, x_ref, w1_ref, w2_ref, o_ref, acc_ref):
    k = pl.program_id(0)

    @pl.when(k == 0)
    def _():
        acc_ref[...] = jnp.zeros_like(acc_ref)

    w1 = w1_ref[...]
    w2 = w2_ref[...]
    for r in range(x_ref.shape[0] // rows_per_step):
        rows = pl.ds(r * rows_per_step, rows_per_step)
        h = jnp.dot(x_ref[rows, :], w1, preferred_element_type=jnp.float32)
        g = (h * 0.5 * (1.0 + lax.erf(h * (2.0 ** -0.5)))).astype(jnp.bfloat16)
        acc_ref[rows, :] += jnp.dot(g, w2, preferred_element_type=jnp.float32)

    @pl.when(k == pl.num_programs(0) - 1)
    def _():
        o_ref[...] = acc_ref[...].astype(o_ref.dtype)


def feed_forward(x, expand, contract, hidden_step=512, rows_per_step=512):
    length, width = x.shape
    hidden = expand.shape[1]
    return pl.pallas_call(
        functools.partial(_feed_forward_kernel, rows_per_step),
        out_shape=jax.ShapeDtypeStruct((length, width), jnp.bfloat16),
        grid=(hidden // hidden_step,),
        in_specs=[
            pl.BlockSpec((length, width), lambda k: (0, 0)),
            pl.BlockSpec((width, hidden_step), lambda k: (0, k)),
            pl.BlockSpec((hidden_step, width), lambda k: (k, 0)),
        ],
        out_specs=pl.BlockSpec((length, width), lambda k: (0, 0)),
        scratch_shapes=[pltpu.VMEM((length, width), jnp.float32)],
        cost_estimate=pl.CostEstimate(
            flops=4 * length * width * hidden,
            transcendentals=length * hidden,
            bytes_accessed=2 * (2 * width * hidden + 2 * length * width),
        ),
    )(x, expand, contract)


def _merge_kernel(res_ref, mine_ref, other_ref, w_ref, o_ref):
    images, cells, width = res_ref.shape
    half = GRID // 2
    slots = half * half
    encoded = jnp.concatenate(
        [
            (res_ref[i] + (mine_ref[i].astype(jnp.float32) + other_ref[i].astype(jnp.float32))).astype(
                jnp.bfloat16
            )
            for i in range(images)
        ],
        axis=0,
    )
    slot = lax.broadcasted_iota(jnp.int32, (images * slots, images * cells), 0)
    cell = lax.broadcasted_iota(jnp.int32, (images * slots, images * cells), 1)
    image = slot // slots
    block = slot % slots
    total = None
    for a in range(2):
        for b in range(2):
            wanted = image * cells + (2 * (block // half) + a) * GRID + 2 * (block % half) + b
            pick = jnp.where(cell == wanted, 1.0, 0.0).astype(jnp.bfloat16)
            rows = jnp.dot(pick, encoded, preferred_element_type=jnp.float32).astype(jnp.bfloat16)
            part = jnp.dot(
                rows,
                w_ref[pl.ds((2 * a + b) * width, width), :],
                preferred_element_type=jnp.float32,
            )
            total = part if total is None else total + part
    for i in range(images):
        o_ref[i] = total[i * slots : (i + 1) * slots].astype(o_ref.dtype)


def merge(residual, mine, other, merge_weight):
    images, cells, width = residual.shape
    half = GRID // 2
    out_width = merge_weight.shape[1]
    return pl.pallas_call(
        _merge_kernel,
        out_shape=jax.ShapeDtypeStruct((images, half * half, out_width), jnp.bfloat16),
        cost_estimate=pl.CostEstimate(
            flops=2 * images * cells * width * (out_width + half * half),
            transcendentals=0,
            bytes_accessed=images * cells * width * 8 + merge_weight.size * 2,
        ),
    )(residual, mine, other, merge_weight)


def _attention_kernel(causal, x_ref, gain_ref, w_ref, valid_ref, wo_ref, o_ref, q_ref, k_ref, v_ref, acc_ref):
    length, width = q_ref.shape
    window = 256
    values = x_ref[0].astype(jnp.float32)
    center = values - jnp.mean(values, axis=-1, keepdims=True)
    spread = jnp.mean(center * center, axis=-1, keepdims=True)
    first = (center * lax.rsqrt(spread + 1e-06) * gain_ref[...]).astype(jnp.bfloat16)
    for j, ref in enumerate((q_ref, k_ref, v_ref)):
        ref[...] = jnp.dot(first, w_ref[j], preferred_element_type=jnp.float32).astype(ref.dtype)
    keys = valid_ref[0] > 0
    if causal:
        row = lax.broadcasted_iota(jnp.int32, (length, length), 0)
        col = lax.broadcasted_iota(jnp.int32, (length, length), 1)
        allowed = keys & (col <= row)
    else:
        allowed = jnp.broadcast_to(keys, (length, length))
    acc_ref[...] = jnp.zeros_like(acc_ref)
    for h in range(width // HEAD_DIM):
        start = min((h * HEAD_DIM) // 128 * 128, width - window)
        lanes = pl.ds(start, window)
        lane = lax.broadcasted_iota(jnp.int32, (1, window), 1) + start
        mine = (lane >= h * HEAD_DIM) & (lane < (h + 1) * HEAD_DIM)
        zero = jnp.zeros((), q_ref.dtype)
        queries = jnp.where(mine, q_ref[:, lanes], zero)
        scores = lax.dot_general(
            queries, k_ref[:, lanes], (((1,), (1,)), ((), ())),
            preferred_element_type=jnp.float32,
        ) * HEAD_DIM ** (-0.5)
        scores = jnp.where(allowed, scores, jnp.float32(-1e30))
        top = jnp.max(scores, axis=-1, keepdims=True)
        raised = jnp.exp(scores - top)
        probs = (raised / jnp.sum(raised, axis=-1, keepdims=True)).astype(jnp.bfloat16)
        values_h = jnp.where(mine, v_ref[:, lanes], zero)
        acc_ref[:, lanes] += jnp.dot(probs, values_h, preferred_element_type=jnp.float32)
    mixed = acc_ref[...].astype(jnp.bfloat16)
    o_ref[0] = jnp.dot(mixed, wo_ref[...], preferred_element_type=jnp.float32).astype(o_ref.dtype)


def attend(inputs, gain_first, attend_in, key_valid, causal, attend_out):
    batch, length, model_width = inputs.shape
    width = attend_in.shape[2]
    weight = jnp.transpose(attend_in, (1, 0, 2))
    mixed = pl.pallas_call(
        functools.partial(_attention_kernel, causal),
        out_shape=jax.ShapeDtypeStruct((batch, length, model_width), jnp.bfloat16),
        grid=(batch,),
        in_specs=[
            pl.BlockSpec((1, length, model_width), lambda b: (b, 0, 0)),
            pl.BlockSpec((1, model_width), lambda b: (0, 0)),
            pl.BlockSpec((3, model_width, width), lambda b: (0, 0, 0)),
            pl.BlockSpec((1, 1, length), lambda b: (b, 0, 0)),
            pl.BlockSpec((width, model_width), lambda b: (0, 0)),
        ],
        out_specs=pl.BlockSpec((1, length, model_width), lambda b: (b, 0, 0)),
        scratch_shapes=[pltpu.VMEM((length, width), jnp.bfloat16)] * 3
        + [pltpu.VMEM((length, width), jnp.float32)],
        cost_estimate=pl.CostEstimate(
            flops=batch * length * (8 * model_width * width + 4 * length * 256 * (width // HEAD_DIM)),
            transcendentals=batch * length * length * (width // HEAD_DIM),
            bytes_accessed=2 * (2 * batch * length * model_width + 4 * model_width * width),
        ),
    )(
        inputs,
        gain_first.reshape(1, model_width),
        weight,
        key_valid.astype(jnp.int32).reshape(batch, 1, length),
        attend_out,
    )
    return mixed


def layer(inputs, key_valid, causal, attend_in, attend_out, expand, contract, gain_first, gain_second, split=False):
    widened = inputs.astype(jnp.float32)
    attended = attend(inputs, gain_first, attend_in, key_valid, causal, attend_out)
    residual = widened + tensor_sum(attended)
    second = normalize(residual, gain_second).astype(jnp.bfloat16)
    batch, length, width = second.shape
    partial_out = feed_forward(second.reshape(batch * length, width), expand, contract)
    mine = partial_out.reshape(batch, length, width)
    other = lax.ppermute(mine, "tensor", [(0, 1), (1, 0)])
    if split:
        return residual, mine, other
    return (residual + (mine.astype(jnp.float32) + other.astype(jnp.float32))).astype(jnp.bfloat16)


def on_device(
    req_count,
    patches,
    grids,
    place,
    text_tokens,
    encoder_attend_in,
    encoder_attend_out,
    encoder_expand,
    encoder_contract,
    encoder_gain_first,
    encoder_gain_second,
    merge_weight,
    decoder_attend_in,
    decoder_attend_out,
    decoder_expand,
    decoder_contract,
    decoder_gain_first,
    decoder_gain_second,
):
    device = lax.axis_index("req")
    core = lax.axis_index("tensor")
    images_here, cell_count, width = patches.shape
    side = GRID
    half = side // 2
    slot_count = half * half
    local_grids = lax.dynamic_slice_in_dim(grids, device * images_here, images_here, 0)
    cells = jnp.arange(cell_count)
    cell_valid = ((cells // side)[None, :] < local_grids[:, 0:1]) & (
        (cells % side)[None, :] < local_grids[:, 1:2]
    )
    residual, mine, other = layer(
        patches,
        cell_valid,
        False,
        encoder_attend_in,
        encoder_attend_out,
        encoder_expand,
        encoder_contract,
        encoder_gain_first,
        encoder_gain_second,
        split=True,
    )
    merged = merge(residual, mine, other, merge_weight)

    swap_pair = [(0, 1), (1, 0)]
    given = lax.ppermute(jnp.where(core == 0, merged[1], merged[0]), "tensor", swap_pair)
    own_image = jnp.where(
        core == 0,
        jnp.concatenate([merged[0], given], axis=-1),
        jnp.concatenate([given, merged[1]], axis=-1),
    )
    sent = []
    for flip in (0, 1):
        perm = [
            (r * 2 + t, (r ^ REQ_XOR[t]) * 2 + (t ^ flip))
            for r in range(req_count)
            for t in range(2)
        ]
        sent.append(lax.ppermute(own_image, ("req", "tensor"), perm))
    arrived = [
        jnp.where(core == 0, sent[0], sent[1]),
        jnp.where(core == 0, sent[1], sent[0]),
    ]
    sources = [(device ^ REQ_XOR[j]) * images_here + j for j in range(images_here)]
    first_slot = place[sources[0]] % 2
    swap = first_slot != 0
    image_rows = jnp.where(
        swap,
        jnp.concatenate([arrived[1], arrived[0]], axis=0),
        jnp.concatenate([arrived[0], arrived[1]], axis=0),
    )
    grid_a = grids[sources[0]]
    grid_b = grids[sources[1]]
    slot_grids = jnp.where(swap, jnp.stack([grid_b, grid_a]), jnp.stack([grid_a, grid_b]))
    slots = jnp.arange(slot_count)
    merged_valid = ((2 * (slots // half))[None, :] < slot_grids[:, 0:1]) & (
        (2 * (slots % half))[None, :] < slot_grids[:, 1:2]
    )
    prompt = jnp.concatenate([image_rows, text_tokens[0]], axis=0)[None]
    text_count = text_tokens.shape[1]
    prompt_valid = jnp.concatenate(
        [merged_valid.reshape(-1), jnp.ones((text_count,), bool)], axis=0
    )
    decoded = layer(
        prompt,
        prompt_valid[None],
        True,
        decoder_attend_in,
        decoder_attend_out,
        decoder_expand,
        decoder_contract,
        decoder_gain_first,
        decoder_gain_second,
    )
    return jnp.where(prompt_valid[None, :, None], decoded, jnp.zeros_like(decoded))


def solution(mesh):
    placed = (
        P("req", None, None),
        P(),
        P(),
        P("req", None, None),
        P(None, None, "tensor"),
        P("tensor", None),
        P(None, "tensor"),
        P("tensor", None),
        P(),
        P(),
        P(None, "tensor"),
        P(None, None, "tensor"),
        P("tensor", None),
        P(None, "tensor"),
        P("tensor", None),
        P(),
        P(),
    )

    def body(*args):
        return on_device(mesh.shape["req"], *args)

    return jax.shard_map(
        body, mesh=mesh, in_specs=placed, out_specs=P("req", None, None), check_vma=False
    )
```

```python
import functools

import jax
import jax.numpy as jnp
from jax import lax
from jax.experimental import pallas as pl
from jax.experimental.pallas import tpu as pltpu
from jax.sharding import PartitionSpec as P

HEAD_DIM = 80
GRID = 16
REQ_XOR = (1, 64)


def normalize(values, gain):
    center = values - jnp.mean(values, axis=-1, keepdims=True)
    spread = jnp.mean(center * center, axis=-1, keepdims=True)
    return center * lax.rsqrt(spread + 1e-06) * gain


def tensor_sum(partial):
    mine = partial.astype(jnp.bfloat16)
    other = lax.ppermute(mine, "tensor", [(0, 1), (1, 0)])
    return mine.astype(jnp.float32) + other.astype(jnp.float32)


def _feed_forward_kernel(rows_per_step, x_ref, w1_ref, w2_ref, o_ref, acc_ref):
    k = pl.program_id(0)

    @pl.when(k == 0)
    def _():
        acc_ref[...] = jnp.zeros_like(acc_ref)

    w1 = w1_ref[...]
    w2 = w2_ref[...]
    for r in range(x_ref.shape[0] // rows_per_step):
        rows = pl.ds(r * rows_per_step, rows_per_step)
        h = jnp.dot(x_ref[rows, :], w1, preferred_element_type=jnp.float32)
        g = (h * 0.5 * (1.0 + lax.erf(h * (2.0 ** -0.5)))).astype(jnp.bfloat16)
        acc_ref[rows, :] += jnp.dot(g, w2, preferred_element_type=jnp.float32)

    @pl.when(k == pl.num_programs(0) - 1)
    def _():
        o_ref[...] = acc_ref[...].astype(o_ref.dtype)


def feed_forward(x, expand, contract, hidden_step=512, rows_per_step=512):
    length, width = x.shape
    hidden = expand.shape[1]
    return pl.pallas_call(
        functools.partial(_feed_forward_kernel, rows_per_step),
        out_shape=jax.ShapeDtypeStruct((length, width), jnp.bfloat16),
        grid=(hidden // hidden_step,),
        in_specs=[
            pl.BlockSpec((length, width), lambda k: (0, 0)),
            pl.BlockSpec((width, hidden_step), lambda k: (0, k)),
            pl.BlockSpec((hidden_step, width), lambda k: (k, 0)),
        ],
        out_specs=pl.BlockSpec((length, width), lambda k: (0, 0)),
        scratch_shapes=[pltpu.VMEM((length, width), jnp.float32)],
        cost_estimate=pl.CostEstimate(
            flops=4 * length * width * hidden,
            transcendentals=length * hidden,
            bytes_accessed=2 * (2 * width * hidden + 2 * length * width),
        ),
    )(x, expand, contract)


def _merge_kernel(res_ref, mine_ref, other_ref, w_ref, o_ref):
    images, cells, width = res_ref.shape
    half = GRID // 2
    slots = half * half
    encoded = jnp.concatenate(
        [
            (res_ref[i] + (mine_ref[i].astype(jnp.float32) + other_ref[i].astype(jnp.float32))).astype(
                jnp.bfloat16
            )
            for i in range(images)
        ],
        axis=0,
    )
    slot = lax.broadcasted_iota(jnp.int32, (images * slots, images * cells), 0)
    cell = lax.broadcasted_iota(jnp.int32, (images * slots, images * cells), 1)
    image = slot // slots
    block = slot % slots
    total = None
    for a in range(2):
        for b in range(2):
            wanted = image * cells + (2 * (block // half) + a) * GRID + 2 * (block % half) + b
            pick = jnp.where(cell == wanted, 1.0, 0.0).astype(jnp.bfloat16)
            rows = jnp.dot(pick, encoded, preferred_element_type=jnp.float32).astype(jnp.bfloat16)
            part = jnp.dot(
                rows,
                w_ref[pl.ds((2 * a + b) * width, width), :],
                preferred_element_type=jnp.float32,
            )
            total = part if total is None else total + part
    for i in range(images):
        o_ref[i] = total[i * slots : (i + 1) * slots].astype(o_ref.dtype)


def merge(residual, mine, other, merge_weight):
    images, cells, width = residual.shape
    half = GRID // 2
    out_width = merge_weight.shape[1]
    return pl.pallas_call(
        _merge_kernel,
        out_shape=jax.ShapeDtypeStruct((images, half * half, out_width), jnp.bfloat16),
        cost_estimate=pl.CostEstimate(
            flops=2 * images * cells * width * (out_width + half * half),
            transcendentals=0,
            bytes_accessed=images * cells * width * 8 + merge_weight.size * 2,
        ),
    )(residual, mine, other, merge_weight)


def _attention_kernel(causal, x_ref, gain_ref, w_ref, valid_ref, wo_ref, o_ref, q_ref, k_ref, v_ref, acc_ref):
    length, width = q_ref.shape
    window = 256
    values = x_ref[0].astype(jnp.float32)
    center = values - jnp.mean(values, axis=-1, keepdims=True)
    spread = jnp.mean(center * center, axis=-1, keepdims=True)
    first = (center * lax.rsqrt(spread + 1e-06) * gain_ref[...]).astype(jnp.bfloat16)
    for j, ref in enumerate((q_ref, k_ref, v_ref)):
        ref[...] = jnp.dot(first, w_ref[j], preferred_element_type=jnp.float32).astype(ref.dtype)
    keys = valid_ref[0] > 0
    blocks = 2 if causal else 1
    block = length // blocks
    allowed = []
    for qi in range(blocks):
        seen = (qi + 1) * block if causal else length
        if causal:
            row = lax.broadcasted_iota(jnp.int32, (block, seen), 0) + qi * block
            col = lax.broadcasted_iota(jnp.int32, (block, seen), 1)
            allowed.append(keys[:, :seen] & (col <= row))
        else:
            allowed.append(jnp.broadcast_to(keys, (block, seen)))
    acc_ref[...] = jnp.zeros_like(acc_ref)
    for h in range(width // HEAD_DIM):
        start = min((h * HEAD_DIM) // 128 * 128, width - window)
        lanes = pl.ds(start, window)
        lane = lax.broadcasted_iota(jnp.int32, (1, window), 1) + start
        mine = (lane >= h * HEAD_DIM) & (lane < (h + 1) * HEAD_DIM)
        zero = jnp.zeros((), q_ref.dtype)
        for qi in range(blocks):
            seen = (qi + 1) * block if causal else length
            rows = pl.ds(qi * block, block)
            queries = jnp.where(mine, q_ref[rows, lanes], zero)
            scores = lax.dot_general(
                queries, k_ref[pl.ds(0, seen), lanes], (((1,), (1,)), ((), ())),
                preferred_element_type=jnp.float32,
            ) * HEAD_DIM ** (-0.5)
            scores = jnp.where(allowed[qi], scores, jnp.float32(-1e30))
            top = jnp.max(scores, axis=-1, keepdims=True)
            raised = jnp.exp(scores - top)
            probs = (raised / jnp.sum(raised, axis=-1, keepdims=True)).astype(jnp.bfloat16)
            values_h = jnp.where(mine, v_ref[pl.ds(0, seen), lanes], zero)
            acc_ref[rows, lanes] += jnp.dot(probs, values_h, preferred_element_type=jnp.float32)
    mixed = acc_ref[...].astype(jnp.bfloat16)
    o_ref[0] = jnp.dot(mixed, wo_ref[...], preferred_element_type=jnp.float32).astype(o_ref.dtype)


def attend(inputs, gain_first, attend_in, key_valid, causal, attend_out):
    batch, length, model_width = inputs.shape
    width = attend_in.shape[2]
    weight = jnp.transpose(attend_in, (1, 0, 2))
    mixed = pl.pallas_call(
        functools.partial(_attention_kernel, causal),
        out_shape=jax.ShapeDtypeStruct((batch, length, model_width), jnp.bfloat16),
        grid=(batch,),
        in_specs=[
            pl.BlockSpec((1, length, model_width), lambda b: (b, 0, 0)),
            pl.BlockSpec((1, model_width), lambda b: (0, 0)),
            pl.BlockSpec((3, model_width, width), lambda b: (0, 0, 0)),
            pl.BlockSpec((1, 1, length), lambda b: (b, 0, 0)),
            pl.BlockSpec((width, model_width), lambda b: (0, 0)),
        ],
        out_specs=pl.BlockSpec((1, length, model_width), lambda b: (b, 0, 0)),
        scratch_shapes=[pltpu.VMEM((length, width), jnp.bfloat16)] * 3
        + [pltpu.VMEM((length, width), jnp.float32)],
        cost_estimate=pl.CostEstimate(
            flops=batch * length * (8 * model_width * width + 4 * length * 256 * (width // HEAD_DIM)),
            transcendentals=batch * length * length * (width // HEAD_DIM),
            bytes_accessed=2 * (2 * batch * length * model_width + 4 * model_width * width),
        ),
    )(
        inputs,
        gain_first.reshape(1, model_width),
        weight,
        key_valid.astype(jnp.int32).reshape(batch, 1, length),
        attend_out,
    )
    return mixed


def layer(inputs, key_valid, causal, attend_in, attend_out, expand, contract, gain_first, gain_second, split=False):
    widened = inputs.astype(jnp.float32)
    attended = attend(inputs, gain_first, attend_in, key_valid, causal, attend_out)
    residual = widened + tensor_sum(attended)
    second = normalize(residual, gain_second).astype(jnp.bfloat16)
    batch, length, width = second.shape
    partial_out = feed_forward(second.reshape(batch * length, width), expand, contract)
    mine = partial_out.reshape(batch, length, width)
    other = lax.ppermute(mine, "tensor", [(0, 1), (1, 0)])
    if split:
        return residual, mine, other
    return (residual + (mine.astype(jnp.float32) + other.astype(jnp.float32))).astype(jnp.bfloat16)


def on_device(
    req_count,
    patches,
    grids,
    place,
    text_tokens,
    encoder_attend_in,
    encoder_attend_out,
    encoder_expand,
    encoder_contract,
    encoder_gain_first,
    encoder_gain_second,
    merge_weight,
    decoder_attend_in,
    decoder_attend_out,
    decoder_expand,
    decoder_contract,
    decoder_gain_first,
    decoder_gain_second,
):
    device = lax.axis_index("req")
    core = lax.axis_index("tensor")
    images_here, cell_count, width = patches.shape
    side = GRID
    half = side // 2
    slot_count = half * half
    local_grids = lax.dynamic_slice_in_dim(grids, device * images_here, images_here, 0)
    cells = jnp.arange(cell_count)
    cell_valid = ((cells // side)[None, :] < local_grids[:, 0:1]) & (
        (cells % side)[None, :] < local_grids[:, 1:2]
    )
    residual, mine, other = layer(
        patches,
        cell_valid,
        False,
        encoder_attend_in,
        encoder_attend_out,
        encoder_expand,
        encoder_contract,
        encoder_gain_first,
        encoder_gain_second,
        split=True,
    )
    merged = merge(residual, mine, other, merge_weight)

    swap_pair = [(0, 1), (1, 0)]
    given = lax.ppermute(jnp.where(core == 0, merged[1], merged[0]), "tensor", swap_pair)
    own_image = jnp.where(
        core == 0,
        jnp.concatenate([merged[0], given], axis=-1),
        jnp.concatenate([given, merged[1]], axis=-1),
    )
    sent = []
    for flip in (0, 1):
        perm = [
            (r * 2 + t, (r ^ REQ_XOR[t]) * 2 + (t ^ flip))
            for r in range(req_count)
            for t in range(2)
        ]
        sent.append(lax.ppermute(own_image, ("req", "tensor"), perm))
    arrived = [
        jnp.where(core == 0, sent[0], sent[1]),
        jnp.where(core == 0, sent[1], sent[0]),
    ]
    sources = [(device ^ REQ_XOR[j]) * images_here + j for j in range(images_here)]
    first_slot = place[sources[0]] % 2
    swap = first_slot != 0
    image_rows = jnp.where(
        swap,
        jnp.concatenate([arrived[1], arrived[0]], axis=0),
        jnp.concatenate([arrived[0], arrived[1]], axis=0),
    )
    grid_a = grids[sources[0]]
    grid_b = grids[sources[1]]
    slot_grids = jnp.where(swap, jnp.stack([grid_b, grid_a]), jnp.stack([grid_a, grid_b]))
    slots = jnp.arange(slot_count)
    merged_valid = ((2 * (slots // half))[None, :] < slot_grids[:, 0:1]) & (
        (2 * (slots % half))[None, :] < slot_grids[:, 1:2]
    )
    prompt = jnp.concatenate([image_rows, text_tokens[0]], axis=0)[None]
    text_count = text_tokens.shape[1]
    prompt_valid = jnp.concatenate(
        [merged_valid.reshape(-1), jnp.ones((text_count,), bool)], axis=0
    )
    decoded = layer(
        prompt,
        prompt_valid[None],
        True,
        decoder_attend_in,
        decoder_attend_out,
        decoder_expand,
        decoder_contract,
        decoder_gain_first,
        decoder_gain_second,
    )
    return jnp.where(prompt_valid[None, :, None], decoded, jnp.zeros_like(decoded))


def solution(mesh):
    placed = (
        P("req", None, None),
        P(),
        P(),
        P("req", None, None),
        P(None, None, "tensor"),
        P("tensor", None),
        P(None, "tensor"),
        P("tensor", None),
        P(),
        P(),
        P(None, "tensor"),
        P(None, None, "tensor"),
        P("tensor", None),
        P(None, "tensor"),
        P("tensor", None),
        P(),
        P(),
    )

    def body(*args):
        return on_device(mesh.shape["req"], *args)

    return jax.shard_map(
        body, mesh=mesh, in_specs=placed, out_specs=P("req", None, None), check_vma=False
    )
```

```python
import functools

import jax
import jax.numpy as jnp
from jax import lax
from jax.experimental import pallas as pl
from jax.experimental.pallas import tpu as pltpu
from jax.sharding import PartitionSpec as P

HEAD_DIM = 80
GRID = 16
REQ_XOR = (1, 64)


def normalize(values, gain):
    center = values - jnp.mean(values, axis=-1, keepdims=True)
    spread = jnp.mean(center * center, axis=-1, keepdims=True)
    return center * lax.rsqrt(spread + 1e-06) * gain


def tensor_sum(partial):
    mine = partial.astype(jnp.bfloat16)
    other = lax.ppermute(mine, "tensor", [(0, 1), (1, 0)])
    return mine.astype(jnp.float32) + other.astype(jnp.float32)


def _feed_forward_kernel(rows_per_step, x_ref, w1_ref, w2_ref, o_ref, acc_ref):
    k = pl.program_id(0)

    @pl.when(k == 0)
    def _():
        acc_ref[...] = jnp.zeros_like(acc_ref)

    w1 = w1_ref[...]
    w2 = w2_ref[...]
    for r in range(x_ref.shape[0] // rows_per_step):
        rows = pl.ds(r * rows_per_step, rows_per_step)
        h = jnp.dot(x_ref[rows, :], w1, preferred_element_type=jnp.float32)
        g = (h * 0.5 * (1.0 + lax.erf(h * (2.0 ** -0.5)))).astype(jnp.bfloat16)
        acc_ref[rows, :] += jnp.dot(g, w2, preferred_element_type=jnp.float32)

    @pl.when(k == pl.num_programs(0) - 1)
    def _():
        o_ref[...] = acc_ref[...].astype(o_ref.dtype)


def feed_forward(x, expand, contract, hidden_step=512, rows_per_step=512):
    length, width = x.shape
    hidden = expand.shape[1]
    return pl.pallas_call(
        functools.partial(_feed_forward_kernel, rows_per_step),
        out_shape=jax.ShapeDtypeStruct((length, width), jnp.bfloat16),
        grid=(hidden // hidden_step,),
        in_specs=[
            pl.BlockSpec((length, width), lambda k: (0, 0)),
            pl.BlockSpec((width, hidden_step), lambda k: (0, k)),
            pl.BlockSpec((hidden_step, width), lambda k: (k, 0)),
        ],
        out_specs=pl.BlockSpec((length, width), lambda k: (0, 0)),
        scratch_shapes=[pltpu.VMEM((length, width), jnp.float32)],
        cost_estimate=pl.CostEstimate(
            flops=4 * length * width * hidden,
            transcendentals=length * hidden,
            bytes_accessed=2 * (2 * width * hidden + 2 * length * width),
        ),
    )(x, expand, contract)


def _merge_kernel(res_ref, mine_ref, other_ref, w_ref, o_ref):
    images, cells, width = res_ref.shape
    half = GRID // 2
    slots = half * half
    encoded = jnp.concatenate(
        [
            (res_ref[i] + (mine_ref[i].astype(jnp.float32) + other_ref[i].astype(jnp.float32))).astype(
                jnp.bfloat16
            )
            for i in range(images)
        ],
        axis=0,
    )
    slot = lax.broadcasted_iota(jnp.int32, (images * slots, images * cells), 0)
    cell = lax.broadcasted_iota(jnp.int32, (images * slots, images * cells), 1)
    image = slot // slots
    block = slot % slots
    total = None
    for a in range(2):
        for b in range(2):
            wanted = image * cells + (2 * (block // half) + a) * GRID + 2 * (block % half) + b
            pick = jnp.where(cell == wanted, 1.0, 0.0).astype(jnp.bfloat16)
            rows = jnp.dot(pick, encoded, preferred_element_type=jnp.float32).astype(jnp.bfloat16)
            part = jnp.dot(
                rows,
                w_ref[pl.ds((2 * a + b) * width, width), :],
                preferred_element_type=jnp.float32,
            )
            total = part if total is None else total + part
    for i in range(images):
        o_ref[i] = total[i * slots : (i + 1) * slots].astype(o_ref.dtype)


def merge(residual, mine, other, merge_weight):
    images, cells, width = residual.shape
    half = GRID // 2
    out_width = merge_weight.shape[1]
    return pl.pallas_call(
        _merge_kernel,
        out_shape=jax.ShapeDtypeStruct((images, half * half, out_width), jnp.bfloat16),
        cost_estimate=pl.CostEstimate(
            flops=2 * images * cells * width * (out_width + half * half),
            transcendentals=0,
            bytes_accessed=images * cells * width * 8 + merge_weight.size * 2,
        ),
    )(residual, mine, other, merge_weight)


def _attention_kernel(causal, x_ref, gain_ref, w_ref, valid_ref, wo_ref, o_ref, q_ref, k_ref, v_ref, acc_ref):
    length, width = q_ref.shape
    window = 256
    values = x_ref[0].astype(jnp.float32)
    center = values - jnp.mean(values, axis=-1, keepdims=True)
    spread = jnp.mean(center * center, axis=-1, keepdims=True)
    first = (center * lax.rsqrt(spread + 1e-06) * gain_ref[...][None, :]).astype(jnp.bfloat16)
    for j, ref in enumerate((q_ref, k_ref, v_ref)):
        ref[...] = jnp.dot(first, w_ref[j], preferred_element_type=jnp.float32).astype(ref.dtype)
    keys = valid_ref[0] > 0
    if causal:
        row = lax.broadcasted_iota(jnp.int32, (length, length), 0)
        col = lax.broadcasted_iota(jnp.int32, (length, length), 1)
        allowed = keys & (col <= row)
    else:
        allowed = jnp.broadcast_to(keys, (length, length))
    acc_ref[...] = jnp.zeros_like(acc_ref)
    for h in range(width // HEAD_DIM):
        start = min((h * HEAD_DIM) // 128 * 128, width - window)
        lanes = pl.ds(start, window)
        lane = lax.broadcasted_iota(jnp.int32, (1, window), 1) + start
        mine = (lane >= h * HEAD_DIM) & (lane < (h + 1) * HEAD_DIM)
        zero = jnp.zeros((), q_ref.dtype)
        queries = jnp.where(mine, q_ref[:, lanes], zero)
        scores = lax.dot_general(
            queries, k_ref[:, lanes], (((1,), (1,)), ((), ())),
            preferred_element_type=jnp.float32,
        ) * HEAD_DIM ** (-0.5)
        scores = jnp.where(allowed, scores, jnp.float32(-1e30))
        top = jnp.max(scores, axis=-1, keepdims=True)
        raised = jnp.exp(scores - top)
        probs = (raised / jnp.sum(raised, axis=-1, keepdims=True)).astype(jnp.bfloat16)
        values_h = jnp.where(mine, v_ref[:, lanes], zero)
        acc_ref[:, lanes] += jnp.dot(probs, values_h, preferred_element_type=jnp.float32)
    mixed = acc_ref[...].astype(jnp.bfloat16)
    o_ref[0] = jnp.dot(mixed, wo_ref[...], preferred_element_type=jnp.float32).astype(o_ref.dtype)


def attend(inputs, gain_first, attend_in, key_valid, causal, attend_out):
    batch, length, model_width = inputs.shape
    width = attend_in.shape[2]
    weight = jnp.transpose(attend_in, (1, 0, 2))
    mixed = pl.pallas_call(
        functools.partial(_attention_kernel, causal),
        out_shape=jax.ShapeDtypeStruct((batch, length, model_width), jnp.bfloat16),
        grid=(batch,),
        in_specs=[
            pl.BlockSpec((1, length, model_width), lambda b: (b, 0, 0)),
            pl.BlockSpec((model_width,), lambda b: (0,)),
            pl.BlockSpec((3, model_width, width), lambda b: (0, 0, 0)),
            pl.BlockSpec((1, 1, length), lambda b: (b, 0, 0)),
            pl.BlockSpec((width, model_width), lambda b: (0, 0)),
        ],
        out_specs=pl.BlockSpec((1, length, model_width), lambda b: (b, 0, 0)),
        scratch_shapes=[pltpu.VMEM((length, width), jnp.bfloat16)] * 3
        + [pltpu.VMEM((length, width), jnp.float32)],
        cost_estimate=pl.CostEstimate(
            flops=batch * length * (8 * model_width * width + 4 * length * 256 * (width // HEAD_DIM)),
            transcendentals=batch * length * length * (width // HEAD_DIM),
            bytes_accessed=2 * (2 * batch * length * model_width + 4 * model_width * width),
        ),
    )(
        inputs,
        gain_first,
        weight,
        key_valid.astype(jnp.int32).reshape(batch, 1, length),
        attend_out,
    )
    return mixed


def layer(inputs, key_valid, causal, attend_in, attend_out, expand, contract, gain_first, gain_second, split=False):
    widened = inputs.astype(jnp.float32)
    attended = attend(inputs, gain_first, attend_in, key_valid, causal, attend_out)
    residual = widened + tensor_sum(attended)
    second = normalize(residual, gain_second).astype(jnp.bfloat16)
    batch, length, width = second.shape
    partial_out = feed_forward(second.reshape(batch * length, width), expand, contract)
    mine = partial_out.reshape(batch, length, width)
    other = lax.ppermute(mine, "tensor", [(0, 1), (1, 0)])
    if split:
        return residual, mine, other
    return (residual + (mine.astype(jnp.float32) + other.astype(jnp.float32))).astype(jnp.bfloat16)


def on_device(
    req_count,
    patches,
    grids,
    place,
    text_tokens,
    encoder_attend_in,
    encoder_attend_out,
    encoder_expand,
    encoder_contract,
    encoder_gain_first,
    encoder_gain_second,
    merge_weight,
    decoder_attend_in,
    decoder_attend_out,
    decoder_expand,
    decoder_contract,
    decoder_gain_first,
    decoder_gain_second,
):
    device = lax.axis_index("req")
    core = lax.axis_index("tensor")
    images_here, cell_count, width = patches.shape
    side = GRID
    half = side // 2
    slot_count = half * half
    local_grids = lax.dynamic_slice_in_dim(grids, device * images_here, images_here, 0)
    cells = jnp.arange(cell_count)
    cell_valid = ((cells // side)[None, :] < local_grids[:, 0:1]) & (
        (cells % side)[None, :] < local_grids[:, 1:2]
    )
    residual, mine, other = layer(
        patches,
        cell_valid,
        False,
        encoder_attend_in,
        encoder_attend_out,
        encoder_expand,
        encoder_contract,
        encoder_gain_first,
        encoder_gain_second,
        split=True,
    )
    merged = merge(residual, mine, other, merge_weight)

    swap_pair = [(0, 1), (1, 0)]
    given = lax.ppermute(jnp.where(core == 0, merged[1], merged[0]), "tensor", swap_pair)
    own_image = jnp.where(
        core == 0,
        jnp.concatenate([merged[0], given], axis=-1),
        jnp.concatenate([given, merged[1]], axis=-1),
    )
    sent = []
    for flip in (0, 1):
        perm = [
            (r * 2 + t, (r ^ REQ_XOR[t]) * 2 + (t ^ flip))
            for r in range(req_count)
            for t in range(2)
        ]
        sent.append(lax.ppermute(own_image, ("req", "tensor"), perm))
    arrived = [
        jnp.where(core == 0, sent[0], sent[1]),
        jnp.where(core == 0, sent[1], sent[0]),
    ]
    sources = [(device ^ REQ_XOR[j]) * images_here + j for j in range(images_here)]
    first_slot = place[sources[0]] % 2
    swap = first_slot != 0
    image_rows = jnp.where(
        swap,
        jnp.concatenate([arrived[1], arrived[0]], axis=0),
        jnp.concatenate([arrived[0], arrived[1]], axis=0),
    )
    grid_a = grids[sources[0]]
    grid_b = grids[sources[1]]
    slot_grids = jnp.where(swap, jnp.stack([grid_b, grid_a]), jnp.stack([grid_a, grid_b]))
    slots = jnp.arange(slot_count)
    merged_valid = ((2 * (slots // half))[None, :] < slot_grids[:, 0:1]) & (
        (2 * (slots % half))[None, :] < slot_grids[:, 1:2]
    )
    prompt = jnp.concatenate([image_rows, text_tokens[0]], axis=0)[None]
    text_count = text_tokens.shape[1]
    prompt_valid = jnp.concatenate(
        [merged_valid.reshape(-1), jnp.ones((text_count,), bool)], axis=0
    )
    decoded = layer(
        prompt,
        prompt_valid[None],
        True,
        decoder_attend_in,
        decoder_attend_out,
        decoder_expand,
        decoder_contract,
        decoder_gain_first,
        decoder_gain_second,
    )
    return jnp.where(prompt_valid[None, :, None], decoded, jnp.zeros_like(decoded))


def solution(mesh):
    placed = (
        P("req", None, None),
        P(),
        P(),
        P("req", None, None),
        P(None, None, "tensor"),
        P("tensor", None),
        P(None, "tensor"),
        P("tensor", None),
        P(),
        P(),
        P(None, "tensor"),
        P(None, None, "tensor"),
        P("tensor", None),
        P(None, "tensor"),
        P("tensor", None),
        P(),
        P(),
    )

    def body(*args):
        return on_device(mesh.shape["req"], *args)

    return jax.shard_map(
        body, mesh=mesh, in_specs=placed, out_specs=P("req", None, None), check_vma=False
    )
```

```python
import functools

import jax
import jax.numpy as jnp
from jax import lax
from jax.experimental import pallas as pl
from jax.experimental.pallas import tpu as pltpu
from jax.sharding import PartitionSpec as P

HEAD_DIM = 80
GRID = 16
REQ_XOR = (1, 64)


def normalize(values, gain):
    center = values - jnp.mean(values, axis=-1, keepdims=True)
    spread = jnp.mean(center * center, axis=-1, keepdims=True)
    return center * lax.rsqrt(spread + 1e-06) * gain


def tensor_sum(partial):
    mine = partial.astype(jnp.bfloat16)
    other = lax.ppermute(mine, "tensor", [(0, 1), (1, 0)])
    return mine.astype(jnp.float32) + other.astype(jnp.float32)


def _feed_forward_kernel(rows_per_step, x_ref, w1_ref, w2_ref, o_ref, acc_ref):
    k = pl.program_id(0)

    @pl.when(k == 0)
    def _():
        acc_ref[...] = jnp.zeros_like(acc_ref)

    w1 = w1_ref[...]
    w2 = w2_ref[...]
    for r in range(x_ref.shape[0] // rows_per_step):
        rows = pl.ds(r * rows_per_step, rows_per_step)
        h = jnp.dot(x_ref[rows, :], w1, preferred_element_type=jnp.float32)
        g = (h * 0.5 * (1.0 + lax.erf(h * (2.0 ** -0.5)))).astype(jnp.bfloat16)
        acc_ref[rows, :] += jnp.dot(g, w2, preferred_element_type=jnp.float32)

    @pl.when(k == pl.num_programs(0) - 1)
    def _():
        o_ref[...] = acc_ref[...].astype(o_ref.dtype)


def feed_forward(x, expand, contract, hidden_step=640, rows_per_step=512):
    length, width = x.shape
    hidden = expand.shape[1]
    return pl.pallas_call(
        functools.partial(_feed_forward_kernel, rows_per_step),
        out_shape=jax.ShapeDtypeStruct((length, width), jnp.bfloat16),
        grid=(hidden // hidden_step,),
        in_specs=[
            pl.BlockSpec((length, width), lambda k: (0, 0)),
            pl.BlockSpec((width, hidden_step), lambda k: (0, k)),
            pl.BlockSpec((hidden_step, width), lambda k: (k, 0)),
        ],
        out_specs=pl.BlockSpec((length, width), lambda k: (0, 0)),
        scratch_shapes=[pltpu.VMEM((length, width), jnp.float32)],
        cost_estimate=pl.CostEstimate(
            flops=4 * length * width * hidden,
            transcendentals=length * hidden,
            bytes_accessed=2 * (2 * width * hidden + 2 * length * width),
        ),
    )(x, expand, contract)


def _merge_kernel(res_ref, mine_ref, other_ref, w_ref, o_ref):
    images, cells, width = res_ref.shape
    half = GRID // 2
    slots = half * half
    encoded = jnp.concatenate(
        [
            (res_ref[i] + (mine_ref[i].astype(jnp.float32) + other_ref[i].astype(jnp.float32))).astype(
                jnp.bfloat16
            )
            for i in range(images)
        ],
        axis=0,
    )
    slot = lax.broadcasted_iota(jnp.int32, (images * slots, images * cells), 0)
    cell = lax.broadcasted_iota(jnp.int32, (images * slots, images * cells), 1)
    image = slot // slots
    block = slot % slots
    total = None
    for a in range(2):
        for b in range(2):
            wanted = image * cells + (2 * (block // half) + a) * GRID + 2 * (block % half) + b
            pick = jnp.where(cell == wanted, 1.0, 0.0).astype(jnp.bfloat16)
            rows = jnp.dot(pick, encoded, preferred_element_type=jnp.float32).astype(jnp.bfloat16)
            part = jnp.dot(
                rows,
                w_ref[pl.ds((2 * a + b) * width, width), :],
                preferred_element_type=jnp.float32,
            )
            total = part if total is None else total + part
    for i in range(images):
        o_ref[i] = total[i * slots : (i + 1) * slots].astype(o_ref.dtype)


def merge(residual, mine, other, merge_weight):
    images, cells, width = residual.shape
    half = GRID // 2
    out_width = merge_weight.shape[1]
    return pl.pallas_call(
        _merge_kernel,
        out_shape=jax.ShapeDtypeStruct((images, half * half, out_width), jnp.bfloat16),
        cost_estimate=pl.CostEstimate(
            flops=2 * images * cells * width * (out_width + half * half),
            transcendentals=0,
            bytes_accessed=images * cells * width * 8 + merge_weight.size * 2,
        ),
    )(residual, mine, other, merge_weight)


def _attention_kernel(causal, x_ref, gain_ref, w_ref, valid_ref, wo_ref, o_ref, q_ref, k_ref, v_ref, acc_ref):
    length, width = q_ref.shape
    window = 256
    values = x_ref[0].astype(jnp.float32)
    center = values - jnp.mean(values, axis=-1, keepdims=True)
    spread = jnp.mean(center * center, axis=-1, keepdims=True)
    first = (center * lax.rsqrt(spread + 1e-06) * gain_ref[...][None, :]).astype(jnp.bfloat16)
    for j, ref in enumerate((q_ref, k_ref, v_ref)):
        ref[...] = jnp.dot(first, w_ref[j], preferred_element_type=jnp.float32).astype(ref.dtype)
    keys = valid_ref[0] > 0
    if causal:
        row = lax.broadcasted_iota(jnp.int32, (length, length), 0)
        col = lax.broadcasted_iota(jnp.int32, (length, length), 1)
        allowed = keys & (col <= row)
    else:
        allowed = jnp.broadcast_to(keys, (length, length))
    acc_ref[...] = jnp.zeros_like(acc_ref)
    for h in range(width // HEAD_DIM):
        start = min((h * HEAD_DIM) // 128 * 128, width - window)
        lanes = pl.ds(start, window)
        lane = lax.broadcasted_iota(jnp.int32, (1, window), 1) + start
        mine = (lane >= h * HEAD_DIM) & (lane < (h + 1) * HEAD_DIM)
        zero = jnp.zeros((), q_ref.dtype)
        queries = jnp.where(mine, q_ref[:, lanes], zero)
        scores = lax.dot_general(
            queries, k_ref[:, lanes], (((1,), (1,)), ((), ())),
            preferred_element_type=jnp.float32,
        ) * HEAD_DIM ** (-0.5)
        scores = jnp.where(allowed, scores, jnp.float32(-1e30))
        top = jnp.max(scores, axis=-1, keepdims=True)
        raised = jnp.exp(scores - top)
        probs = (raised / jnp.sum(raised, axis=-1, keepdims=True)).astype(jnp.bfloat16)
        values_h = jnp.where(mine, v_ref[:, lanes], zero)
        acc_ref[:, lanes] += jnp.dot(probs, values_h, preferred_element_type=jnp.float32)
    mixed = acc_ref[...].astype(jnp.bfloat16)
    o_ref[0] = jnp.dot(mixed, wo_ref[...], preferred_element_type=jnp.float32).astype(o_ref.dtype)


def attend(inputs, gain_first, attend_in, key_valid, causal, attend_out):
    batch, length, model_width = inputs.shape
    width = attend_in.shape[2]
    weight = jnp.transpose(attend_in, (1, 0, 2))
    mixed = pl.pallas_call(
        functools.partial(_attention_kernel, causal),
        out_shape=jax.ShapeDtypeStruct((batch, length, model_width), jnp.bfloat16),
        grid=(batch,),
        in_specs=[
            pl.BlockSpec((1, length, model_width), lambda b: (b, 0, 0)),
            pl.BlockSpec((model_width,), lambda b: (0,)),
            pl.BlockSpec((3, model_width, width), lambda b: (0, 0, 0)),
            pl.BlockSpec((1, 1, length), lambda b: (b, 0, 0)),
            pl.BlockSpec((width, model_width), lambda b: (0, 0)),
        ],
        out_specs=pl.BlockSpec((1, length, model_width), lambda b: (b, 0, 0)),
        scratch_shapes=[pltpu.VMEM((length, width), jnp.bfloat16)] * 3
        + [pltpu.VMEM((length, width), jnp.float32)],
        cost_estimate=pl.CostEstimate(
            flops=batch * length * (8 * model_width * width + 4 * length * 256 * (width // HEAD_DIM)),
            transcendentals=batch * length * length * (width // HEAD_DIM),
            bytes_accessed=2 * (2 * batch * length * model_width + 4 * model_width * width),
        ),
    )(
        inputs,
        gain_first,
        weight,
        key_valid.astype(jnp.int32).reshape(batch, 1, length),
        attend_out,
    )
    return mixed


def layer(inputs, key_valid, causal, attend_in, attend_out, expand, contract, gain_first, gain_second, split=False):
    widened = inputs.astype(jnp.float32)
    attended = attend(inputs, gain_first, attend_in, key_valid, causal, attend_out)
    residual = widened + tensor_sum(attended)
    second = normalize(residual, gain_second).astype(jnp.bfloat16)
    batch, length, width = second.shape
    partial_out = feed_forward(second.reshape(batch * length, width), expand, contract)
    mine = partial_out.reshape(batch, length, width)
    other = lax.ppermute(mine, "tensor", [(0, 1), (1, 0)])
    if split:
        return residual, mine, other
    return (residual + (mine.astype(jnp.float32) + other.astype(jnp.float32))).astype(jnp.bfloat16)


def on_device(
    req_count,
    patches,
    grids,
    place,
    text_tokens,
    encoder_attend_in,
    encoder_attend_out,
    encoder_expand,
    encoder_contract,
    encoder_gain_first,
    encoder_gain_second,
    merge_weight,
    decoder_attend_in,
    decoder_attend_out,
    decoder_expand,
    decoder_contract,
    decoder_gain_first,
    decoder_gain_second,
):
    device = lax.axis_index("req")
    core = lax.axis_index("tensor")
    images_here, cell_count, width = patches.shape
    side = GRID
    half = side // 2
    slot_count = half * half
    local_grids = lax.dynamic_slice_in_dim(grids, device * images_here, images_here, 0)
    cells = jnp.arange(cell_count)
    cell_valid = ((cells // side)[None, :] < local_grids[:, 0:1]) & (
        (cells % side)[None, :] < local_grids[:, 1:2]
    )
    residual, mine, other = layer(
        patches,
        cell_valid,
        False,
        encoder_attend_in,
        encoder_attend_out,
        encoder_expand,
        encoder_contract,
        encoder_gain_first,
        encoder_gain_second,
        split=True,
    )
    merged = merge(residual, mine, other, merge_weight)

    swap_pair = [(0, 1), (1, 0)]
    given = lax.ppermute(jnp.where(core == 0, merged[1], merged[0]), "tensor", swap_pair)
    own_image = jnp.where(
        core == 0,
        jnp.concatenate([merged[0], given], axis=-1),
        jnp.concatenate([given, merged[1]], axis=-1),
    )
    sent = []
    for flip in (0, 1):
        perm = [
            (r * 2 + t, (r ^ REQ_XOR[t]) * 2 + (t ^ flip))
            for r in range(req_count)
            for t in range(2)
        ]
        sent.append(lax.ppermute(own_image, ("req", "tensor"), perm))
    arrived = [
        jnp.where(core == 0, sent[0], sent[1]),
        jnp.where(core == 0, sent[1], sent[0]),
    ]
    sources = [(device ^ REQ_XOR[j]) * images_here + j for j in range(images_here)]
    first_slot = place[sources[0]] % 2
    swap = first_slot != 0
    image_rows = jnp.where(
        swap,
        jnp.concatenate([arrived[1], arrived[0]], axis=0),
        jnp.concatenate([arrived[0], arrived[1]], axis=0),
    )
    grid_a = grids[sources[0]]
    grid_b = grids[sources[1]]
    slot_grids = jnp.where(swap, jnp.stack([grid_b, grid_a]), jnp.stack([grid_a, grid_b]))
    slots = jnp.arange(slot_count)
    merged_valid = ((2 * (slots // half))[None, :] < slot_grids[:, 0:1]) & (
        (2 * (slots % half))[None, :] < slot_grids[:, 1:2]
    )
    prompt = jnp.concatenate([image_rows, text_tokens[0]], axis=0)[None]
    text_count = text_tokens.shape[1]
    prompt_valid = jnp.concatenate(
        [merged_valid.reshape(-1), jnp.ones((text_count,), bool)], axis=0
    )
    decoded = layer(
        prompt,
        prompt_valid[None],
        True,
        decoder_attend_in,
        decoder_attend_out,
        decoder_expand,
        decoder_contract,
        decoder_gain_first,
        decoder_gain_second,
    )
    return jnp.where(prompt_valid[None, :, None], decoded, jnp.zeros_like(decoded))


def solution(mesh):
    placed = (
        P("req", None, None),
        P(),
        P(),
        P("req", None, None),
        P(None, None, "tensor"),
        P("tensor", None),
        P(None, "tensor"),
        P("tensor", None),
        P(),
        P(),
        P(None, "tensor"),
        P(None, None, "tensor"),
        P("tensor", None),
        P(None, "tensor"),
        P("tensor", None),
        P(),
        P(),
    )

    def body(*args):
        return on_device(mesh.shape["req"], *args)

    return jax.shard_map(
        body, mesh=mesh, in_specs=placed, out_specs=P("req", None, None), check_vma=False
    )
```

```python
import functools

import jax
import jax.numpy as jnp
from jax import lax
from jax.experimental import pallas as pl
from jax.experimental.pallas import tpu as pltpu
from jax.sharding import PartitionSpec as P

HEAD_DIM = 80
GRID = 16
REQ_XOR = (1, 64)


def normalize(values, gain):
    center = values - jnp.mean(values, axis=-1, keepdims=True)
    spread = jnp.mean(center * center, axis=-1, keepdims=True)
    return center * lax.rsqrt(spread + 1e-06) * gain


def tensor_sum(partial):
    mine = partial.astype(jnp.bfloat16)
    other = lax.ppermute(mine, "tensor", [(0, 1), (1, 0)])
    return mine.astype(jnp.float32) + other.astype(jnp.float32)


def _feed_forward_kernel(rows_per_step, x_ref, w1_ref, w2_ref, o_ref, acc_ref):
    k = pl.program_id(0)

    @pl.when(k == 0)
    def _():
        acc_ref[...] = jnp.zeros_like(acc_ref)

    w1 = w1_ref[...]
    w2 = w2_ref[...]
    for r in range(x_ref.shape[0] // rows_per_step):
        rows = pl.ds(r * rows_per_step, rows_per_step)
        h = jnp.dot(x_ref[rows, :], w1, preferred_element_type=jnp.float32)
        g = (h * 0.5 * (1.0 + lax.erf(h * (2.0 ** -0.5)))).astype(jnp.bfloat16)
        acc_ref[rows, :] += jnp.dot(g, w2, preferred_element_type=jnp.float32)

    @pl.when(k == pl.num_programs(0) - 1)
    def _():
        o_ref[...] = acc_ref[...].astype(o_ref.dtype)


def feed_forward(x, expand, contract, hidden_step=256, rows_per_step=512):
    length, width = x.shape
    hidden = expand.shape[1]
    return pl.pallas_call(
        functools.partial(_feed_forward_kernel, rows_per_step),
        out_shape=jax.ShapeDtypeStruct((length, width), jnp.bfloat16),
        grid=(hidden // hidden_step,),
        in_specs=[
            pl.BlockSpec((length, width), lambda k: (0, 0)),
            pl.BlockSpec((width, hidden_step), lambda k: (0, k)),
            pl.BlockSpec((hidden_step, width), lambda k: (k, 0)),
        ],
        out_specs=pl.BlockSpec((length, width), lambda k: (0, 0)),
        scratch_shapes=[pltpu.VMEM((length, width), jnp.float32)],
        cost_estimate=pl.CostEstimate(
            flops=4 * length * width * hidden,
            transcendentals=length * hidden,
            bytes_accessed=2 * (2 * width * hidden + 2 * length * width),
        ),
    )(x, expand, contract)


def _merge_kernel(res_ref, mine_ref, other_ref, w_ref, o_ref):
    images, cells, width = res_ref.shape
    half = GRID // 2
    slots = half * half
    encoded = jnp.concatenate(
        [
            (res_ref[i] + (mine_ref[i].astype(jnp.float32) + other_ref[i].astype(jnp.float32))).astype(
                jnp.bfloat16
            )
            for i in range(images)
        ],
        axis=0,
    )
    slot = lax.broadcasted_iota(jnp.int32, (images * slots, images * cells), 0)
    cell = lax.broadcasted_iota(jnp.int32, (images * slots, images * cells), 1)
    image = slot // slots
    block = slot % slots
    total = None
    for a in range(2):
        for b in range(2):
            wanted = image * cells + (2 * (block // half) + a) * GRID + 2 * (block % half) + b
            pick = jnp.where(cell == wanted, 1.0, 0.0).astype(jnp.bfloat16)
            rows = jnp.dot(pick, encoded, preferred_element_type=jnp.float32).astype(jnp.bfloat16)
            part = jnp.dot(
                rows,
                w_ref[pl.ds((2 * a + b) * width, width), :],
                preferred_element_type=jnp.float32,
            )
            total = part if total is None else total + part
    for i in range(images):
        o_ref[i] = total[i * slots : (i + 1) * slots].astype(o_ref.dtype)


def merge(residual, mine, other, merge_weight):
    images, cells, width = residual.shape
    half = GRID // 2
    out_width = merge_weight.shape[1]
    return pl.pallas_call(
        _merge_kernel,
        out_shape=jax.ShapeDtypeStruct((images, half * half, out_width), jnp.bfloat16),
        cost_estimate=pl.CostEstimate(
            flops=2 * images * cells * width * (out_width + half * half),
            transcendentals=0,
            bytes_accessed=images * cells * width * 8 + merge_weight.size * 2,
        ),
    )(residual, mine, other, merge_weight)


def _attention_kernel(causal, x_ref, gain_ref, w_ref, valid_ref, wo_ref, o_ref, q_ref, k_ref, v_ref, acc_ref):
    length, width = q_ref.shape
    window = 256
    values = x_ref[0].astype(jnp.float32)
    center = values - jnp.mean(values, axis=-1, keepdims=True)
    spread = jnp.mean(center * center, axis=-1, keepdims=True)
    first = (center * lax.rsqrt(spread + 1e-06) * gain_ref[...][None, :]).astype(jnp.bfloat16)
    for j, ref in enumerate((q_ref, k_ref, v_ref)):
        ref[...] = jnp.dot(first, w_ref[j], preferred_element_type=jnp.float32).astype(ref.dtype)
    keys = valid_ref[0] > 0
    if causal:
        row = lax.broadcasted_iota(jnp.int32, (length, length), 0)
        col = lax.broadcasted_iota(jnp.int32, (length, length), 1)
        allowed = keys & (col <= row)
    else:
        allowed = jnp.broadcast_to(keys, (length, length))
    acc_ref[...] = jnp.zeros_like(acc_ref)
    for h in range(width // HEAD_DIM):
        start = min((h * HEAD_DIM) // 128 * 128, width - window)
        lanes = pl.ds(start, window)
        lane = lax.broadcasted_iota(jnp.int32, (1, window), 1) + start
        mine = (lane >= h * HEAD_DIM) & (lane < (h + 1) * HEAD_DIM)
        zero = jnp.zeros((), q_ref.dtype)
        queries = jnp.where(mine, q_ref[:, lanes], zero)
        scores = lax.dot_general(
            queries, k_ref[:, lanes], (((1,), (1,)), ((), ())),
            preferred_element_type=jnp.float32,
        ) * HEAD_DIM ** (-0.5)
        scores = jnp.where(allowed, scores, jnp.float32(-1e30))
        top = jnp.max(scores, axis=-1, keepdims=True)
        raised = jnp.exp(scores - top)
        probs = (raised / jnp.sum(raised, axis=-1, keepdims=True)).astype(jnp.bfloat16)
        values_h = jnp.where(mine, v_ref[:, lanes], zero)
        acc_ref[:, lanes] += jnp.dot(probs, values_h, preferred_element_type=jnp.float32)
    mixed = acc_ref[...].astype(jnp.bfloat16)
    o_ref[0] = jnp.dot(mixed, wo_ref[...], preferred_element_type=jnp.float32).astype(o_ref.dtype)


def attend(inputs, gain_first, attend_in, key_valid, causal, attend_out):
    batch, length, model_width = inputs.shape
    width = attend_in.shape[2]
    weight = jnp.transpose(attend_in, (1, 0, 2))
    mixed = pl.pallas_call(
        functools.partial(_attention_kernel, causal),
        out_shape=jax.ShapeDtypeStruct((batch, length, model_width), jnp.bfloat16),
        grid=(batch,),
        in_specs=[
            pl.BlockSpec((1, length, model_width), lambda b: (b, 0, 0)),
            pl.BlockSpec((model_width,), lambda b: (0,)),
            pl.BlockSpec((3, model_width, width), lambda b: (0, 0, 0)),
            pl.BlockSpec((1, 1, length), lambda b: (b, 0, 0)),
            pl.BlockSpec((width, model_width), lambda b: (0, 0)),
        ],
        out_specs=pl.BlockSpec((1, length, model_width), lambda b: (b, 0, 0)),
        scratch_shapes=[pltpu.VMEM((length, width), jnp.bfloat16)] * 3
        + [pltpu.VMEM((length, width), jnp.float32)],
        cost_estimate=pl.CostEstimate(
            flops=batch * length * (8 * model_width * width + 4 * length * 256 * (width // HEAD_DIM)),
            transcendentals=batch * length * length * (width // HEAD_DIM),
            bytes_accessed=2 * (2 * batch * length * model_width + 4 * model_width * width),
        ),
    )(
        inputs,
        gain_first,
        weight,
        key_valid.astype(jnp.int32).reshape(batch, 1, length),
        attend_out,
    )
    return mixed


def layer(inputs, key_valid, causal, attend_in, attend_out, expand, contract, gain_first, gain_second, split=False):
    widened = inputs.astype(jnp.float32)
    attended = attend(inputs, gain_first, attend_in, key_valid, causal, attend_out)
    residual = widened + tensor_sum(attended)
    second = normalize(residual, gain_second).astype(jnp.bfloat16)
    batch, length, width = second.shape
    partial_out = feed_forward(second.reshape(batch * length, width), expand, contract)
    mine = partial_out.reshape(batch, length, width)
    other = lax.ppermute(mine, "tensor", [(0, 1), (1, 0)])
    if split:
        return residual, mine, other
    return (residual + (mine.astype(jnp.float32) + other.astype(jnp.float32))).astype(jnp.bfloat16)


def on_device(
    req_count,
    patches,
    grids,
    place,
    text_tokens,
    encoder_attend_in,
    encoder_attend_out,
    encoder_expand,
    encoder_contract,
    encoder_gain_first,
    encoder_gain_second,
    merge_weight,
    decoder_attend_in,
    decoder_attend_out,
    decoder_expand,
    decoder_contract,
    decoder_gain_first,
    decoder_gain_second,
):
    device = lax.axis_index("req")
    core = lax.axis_index("tensor")
    images_here, cell_count, width = patches.shape
    side = GRID
    half = side // 2
    slot_count = half * half
    local_grids = lax.dynamic_slice_in_dim(grids, device * images_here, images_here, 0)
    cells = jnp.arange(cell_count)
    cell_valid = ((cells // side)[None, :] < local_grids[:, 0:1]) & (
        (cells % side)[None, :] < local_grids[:, 1:2]
    )
    residual, mine, other = layer(
        patches,
        cell_valid,
        False,
        encoder_attend_in,
        encoder_attend_out,
        encoder_expand,
        encoder_contract,
        encoder_gain_first,
        encoder_gain_second,
        split=True,
    )
    merged = merge(residual, mine, other, merge_weight)

    swap_pair = [(0, 1), (1, 0)]
    given = lax.ppermute(jnp.where(core == 0, merged[1], merged[0]), "tensor", swap_pair)
    own_image = jnp.where(
        core == 0,
        jnp.concatenate([merged[0], given], axis=-1),
        jnp.concatenate([given, merged[1]], axis=-1),
    )
    sent = []
    for flip in (0, 1):
        perm = [
            (r * 2 + t, (r ^ REQ_XOR[t]) * 2 + (t ^ flip))
            for r in range(req_count)
            for t in range(2)
        ]
        sent.append(lax.ppermute(own_image, ("req", "tensor"), perm))
    arrived = [
        jnp.where(core == 0, sent[0], sent[1]),
        jnp.where(core == 0, sent[1], sent[0]),
    ]
    sources = [(device ^ REQ_XOR[j]) * images_here + j for j in range(images_here)]
    first_slot = place[sources[0]] % 2
    swap = first_slot != 0
    image_rows = jnp.where(
        swap,
        jnp.concatenate([arrived[1], arrived[0]], axis=0),
        jnp.concatenate([arrived[0], arrived[1]], axis=0),
    )
    grid_a = grids[sources[0]]
    grid_b = grids[sources[1]]
    slot_grids = jnp.where(swap, jnp.stack([grid_b, grid_a]), jnp.stack([grid_a, grid_b]))
    slots = jnp.arange(slot_count)
    merged_valid = ((2 * (slots // half))[None, :] < slot_grids[:, 0:1]) & (
        (2 * (slots % half))[None, :] < slot_grids[:, 1:2]
    )
    prompt = jnp.concatenate([image_rows, text_tokens[0]], axis=0)[None]
    text_count = text_tokens.shape[1]
    prompt_valid = jnp.concatenate(
        [merged_valid.reshape(-1), jnp.ones((text_count,), bool)], axis=0
    )
    decoded = layer(
        prompt,
        prompt_valid[None],
        True,
        decoder_attend_in,
        decoder_attend_out,
        decoder_expand,
        decoder_contract,
        decoder_gain_first,
        decoder_gain_second,
    )
    return jnp.where(prompt_valid[None, :, None], decoded, jnp.zeros_like(decoded))


def solution(mesh):
    placed = (
        P("req", None, None),
        P(),
        P(),
        P("req", None, None),
        P(None, None, "tensor"),
        P("tensor", None),
        P(None, "tensor"),
        P("tensor", None),
        P(),
        P(),
        P(None, "tensor"),
        P(None, None, "tensor"),
        P("tensor", None),
        P(None, "tensor"),
        P("tensor", None),
        P(),
        P(),
    )

    def body(*args):
        return on_device(mesh.shape["req"], *args)

    return jax.shard_map(
        body, mesh=mesh, in_specs=placed, out_specs=P("req", None, None), check_vma=False
    )
```
